512 devices in a mesh: chan: 128 (over z, y, core), win: 4 (over x).
Axes of the slice: x: 4, y: 8, z: 8, core: 2. Of those that a mesh axis runs over, the one named last changes fastest.
Arguments:
- records: bfloat16 [16384, 16384], P('chan', 'win'), may hold values from -60 to 60
- offsets: int32 [4], replicated, may hold values from 1 to 15, as said below
- starts: int32 [4], P('win'), may hold values from 0 to 2048
Outputs:
- stacked: float32 [16, 4, 16384, 128], P('win', None, 'chan')
The draws below stay inside these ranges and needn't reach their ends.
Inputs may be any that keep to these rules, and one draw needn't show every extreme that they name: The offsets are distinct, and the largest is 15.
All inputs are finite; a program needn't handle non-finite values.
Results may differ from the reference program's by a relative error of at most 0.006.
Values may be sent and summed in bfloat16 or wider, within the bound.
No kernel may reach another device: no remote copies, remote signals or barrier semaphores. Data moves between devices by JAX's collectives and lax.ppermute only.
A program may use at most 64 MiB of HBM per device.

```python
import math
import jax
import jax.numpy as jnp
from jax import lax

CB = 128
WIN = 2048
NBIN = 1024
BAND = 64
L = 16
K = 4
W_DEV = 1
SEG = 4096
OFFCAP = 16
MAXOFF = 16
NCH = 16384
WINS = 4
TSAMP = 16384
N_CHAN = 128


def draw_records(key, part):
    key_scale, key_base = jax.random.split(jax.random.fold_in(key, 11), 2)
    scale = jnp.exp(jax.random.uniform(key_scale, (NCH, 1), jnp.float32, 0.0, math.log(10.0)))
    base = jnp.clip(jax.random.normal(key_base, (NCH, TSAMP), jnp.float32), -5.0, 5.0)
    return (scale * base).astype(jnp.bfloat16)


def draw_offsets(key, part):
    key_pick, key_order = jax.random.split(jax.random.fold_in(key, 23))
    others = jax.random.permutation(key_pick, MAXOFF - 2)[:K - 1] + 1
    values = jnp.concatenate([others.astype(jnp.int32), jnp.array([MAXOFF - 1], jnp.int32)])
    return jax.random.permutation(key_order, values).astype(jnp.int32)


def set_ends(drawn, stream_key, low, high):
    longest = drawn.shape.index(max(drawn.shape))
    spots = []
    for shift in (0, 1):
        where = [jax.random.randint(jax.random.fold_in(stream_key, axis), (), 0, length) for axis, length in enumerate(drawn.shape)]
        where[longest] = (where[longest] + shift) % drawn.shape[longest]
        spots.append(tuple(where))
    return drawn.at[spots[0]].set(low).at[spots[1]].set(high)


def setup_inputs(seed: int = 0) -> dict:
    key_list = jax.random.split(jax.random.key(seed), 4)
    return {
        "records": draw_records(jax.random.fold_in(key_list[3], 71), 0),
        "offsets": draw_offsets(jax.random.fold_in(key_list[3], 71), 0),
        "starts": set_ends(jax.random.randint(key_list[2], (WINS,), 0, SEG - WIN + 1), jax.random.fold_in(key_list[2], 1), 0, SEG - WIN).astype(jnp.int32),
    }


turn_full = 2.0 * math.pi

def dft_tables():
    samples = jnp.arange(WIN, dtype=jnp.int32)
    bins = jnp.arange(NBIN, dtype=jnp.int32)
    turns = samples[:, None] * bins[None, :] % WIN
    angles = turn_full / WIN * turns.astype(jnp.float32)
    return (jnp.cos(angles).astype(jnp.bfloat16), (-jnp.sin(angles)).astype(jnp.bfloat16))

def taper_weights():
    samples = jnp.arange(WIN, dtype=jnp.float32)
    return 0.5 - 0.5 * jnp.cos(turn_full / WIN * (samples + 0.5))

def band_matrix():
    bins = jnp.arange(NBIN, dtype=jnp.int32)
    near = (jnp.abs(bins[:, None] - bins[None, :]) <= BAND).astype(jnp.float32)
    return near / lax.optimization_barrier(jnp.sum(near, axis=0, keepdims=True))

def phase_tables(windows_total):
    lags = jnp.arange(L, dtype=jnp.int32) - L // 2
    bins = jnp.arange(NBIN, dtype=jnp.int32)
    turns = bins[None, :] * (lags[:, None] + WIN) % WIN
    angles = turn_full / WIN * turns.astype(jnp.float32)
    weight = jnp.where(bins == 0, 1.0, 2.0).astype(jnp.float32) / (2.0 * math.sqrt(NBIN * windows_total))
    return (jnp.cos(angles) * weight[None, :], jnp.sin(angles) * weight[None, :])

def whiten(frames, cos_table, sin_table, taper, band):
    values = frames.astype(jnp.float32)
    shaped = ((values - lax.optimization_barrier(jnp.mean(values, axis=1, keepdims=True))) * taper[None, :]).astype(jnp.bfloat16)
    real = jnp.dot(shaped, cos_table, preferred_element_type=jnp.float32)
    imag = jnp.dot(shaped, sin_table, preferred_element_type=jnp.float32)
    level = jnp.dot(jnp.sqrt(real * real + imag * imag), band, precision=lax.Precision.HIGHEST) + 1e-05
    return ((real / level).astype(jnp.bfloat16), (imag / level).astype(jnp.bfloat16))

def lag_terms(own_re, own_im, partner, cos_w, sin_w):
    ar = own_re.astype(jnp.float32)[:, :, None, :]
    ai = own_im.astype(jnp.float32)[:, :, None, :]
    first = (ar * cos_w[None, None] - ai * sin_w[None, None]).astype(jnp.bfloat16)
    second = (ar * sin_w[None, None] + ai * cos_w[None, None]).astype(jnp.bfloat16)
    part_re = partner[:, :, 0].astype(jnp.float32)
    part_im = partner[:, :, 1].astype(jnp.float32)
    return jnp.einsum('wctf,wkjf->tkcj', first.astype(jnp.float32), part_re) + jnp.einsum('wctf,wkjf->tkcj', second.astype(jnp.float32), part_im)

def reference(records, offsets, starts):
    cos_table, sin_table = dft_tables()
    taper = taper_weights()
    band = band_matrix()
    re_list = []
    im_list = []
    for window in range(WINS):
        begin = window // W_DEV * SEG + starts[window]
        frames = lax.dynamic_slice_in_dim(records, begin.astype(jnp.int32), WIN, 1)
        white_re, white_im = whiten(frames, cos_table, sin_table, taper, band)
        re_list.append(white_re)
        im_list.append(white_im)
    all_re = jnp.stack(re_list, axis=0)
    all_im = jnp.stack(im_list, axis=0)
    padding = jnp.zeros((WINS, OFFCAP * CB, NBIN), jnp.bfloat16)
    padded_re = jnp.concatenate([all_re, padding], axis=1)
    padded_im = jnp.concatenate([all_im, padding], axis=1)
    cos_w, sin_w = phase_tables(WINS)

    def one_block(block):
        first_row = (block * CB).astype(jnp.int32)
        own_re = lax.dynamic_slice_in_dim(all_re, first_row, CB, 1)
        own_im = lax.dynamic_slice_in_dim(all_im, first_row, CB, 1)
        partners = []
        for entry in range(K):
            begin = ((block + offsets[entry]) * CB).astype(jnp.int32)
            piece_re = lax.dynamic_slice_in_dim(padded_re, begin, CB, 1)
            piece_im = lax.dynamic_slice_in_dim(padded_im, begin, CB, 1)
            partners.append(jnp.stack([piece_re, piece_im], axis=1))
        partner = jnp.stack(partners, axis=1)
        return lag_terms(own_re, own_im, partner, cos_w, sin_w)
    blocks = lax.map(one_block, jnp.arange(N_CHAN, dtype=jnp.int32))
    return jnp.transpose(blocks, (1, 2, 0, 3, 4)).reshape(L, K, NCH, CB)
```

```python
import math

import jax
import jax.numpy as jnp
import ml_dtypes
import numpy as np
from jax import lax
from jax.sharding import PartitionSpec as P

WIN = 2048
NBIN = 1024
BAND = 64
L = 16
K = 4
OFFCAP = 16


turn_full = 2.0 * math.pi


def dft_table():
    samples = np.arange(WIN, dtype=np.int64)
    bins = np.arange(NBIN, dtype=np.int64)
    turns = samples[:, None] * bins[None, :] % WIN
    angles = np.float32(turn_full / WIN) * turns.astype(np.float32)
    table = np.concatenate([np.cos(angles), -np.sin(angles)], axis=1)
    return jnp.asarray(table.astype(ml_dtypes.bfloat16))


def taper_weights():
    samples = jnp.arange(WIN, dtype=jnp.float32)
    return 0.5 - 0.5 * jnp.cos(turn_full / WIN * (samples + 0.5))


def band_matrix():
    bins = jnp.arange(NBIN, dtype=jnp.int32)
    near = (jnp.abs(bins[:, None] - bins[None, :]) <= BAND).astype(jnp.float32)
    return near / jnp.sum(near, axis=0, keepdims=True)


def phase_tables(windows_total):
    lags = jnp.arange(L, dtype=jnp.int32) - L // 2
    bins = jnp.arange(NBIN, dtype=jnp.int32)
    turns = bins[None, :] * (lags[:, None] + WIN) % WIN
    angles = turn_full / WIN * turns.astype(jnp.float32)
    weight = jnp.where(bins == 0, 1.0, 2.0).astype(jnp.float32) / (
        2.0 * math.sqrt(NBIN * windows_total)
    )
    return (jnp.cos(angles) * weight[None, :], jnp.sin(angles) * weight[None, :])


def whiten(frames, table, taper, band):
    values = frames.astype(jnp.float32)
    shaped = ((values - jnp.mean(values, axis=1, keepdims=True)) * taper[None, :]).astype(
        jnp.bfloat16
    )
    spec = jnp.dot(shaped, table, preferred_element_type=jnp.float32)
    real = spec[:, :NBIN]
    imag = spec[:, NBIN:]
    level = (
        jnp.dot(jnp.sqrt(real * real + imag * imag), band, precision=lax.Precision.HIGHEST) + 1e-05
    )
    return ((real / level).astype(jnp.bfloat16), (imag / level).astype(jnp.bfloat16))


def lag_terms(own_re, own_im, partner, cos_w, sin_w):
    ar = own_re.astype(jnp.float32)[:, None, :]
    ai = own_im.astype(jnp.float32)[:, None, :]
    first = (ar * cos_w[None] - ai * sin_w[None]).astype(jnp.bfloat16)
    second = (ar * sin_w[None] + ai * cos_w[None]).astype(jnp.bfloat16)
    return jnp.einsum(
        "ctf,kjf->tkcj", first, partner[:, 0], preferred_element_type=jnp.float32
    ) + jnp.einsum("ctf,kjf->tkcj", second, partner[:, 1], preferred_element_type=jnp.float32)


def on_device(records, offsets, starts):
    n_chan = lax.axis_size("chan")
    groups = lax.axis_size("win")
    me = lax.axis_index("chan")
    frames = lax.dynamic_slice_in_dim(records, starts[0], WIN, 1)
    own_re, own_im = whiten(frames, dft_table(), taper_weights(), band_matrix())
    spectra = jnp.stack((own_re, own_im), axis=0)

    down = [(i + 1, i) for i in range(n_chan - 1)]
    jump = [((i + OFFCAP) % n_chan, i) for i in range(n_chan)]
    up = [((i - 1) % n_chan, i) for i in range(n_chan)]

    near = jnp.minimum(offsets, OFFCAP - offsets)
    steps = jnp.max(near)

    def advance(carry):
        step, low, high, picked = carry
        step = step + 1
        low = lax.ppermute(low, "chan", down)
        high = lax.ppermute(high, "chan", up)
        hit_low = offsets == step
        hit_high = offsets == OFFCAP - step
        picked = jnp.where(hit_low[:, None, None, None], low[None], picked)
        picked = jnp.where(hit_high[:, None, None, None], high[None], picked)
        return (step, low, high, picked)

    high0 = lax.ppermute(spectra, "chan", jump)
    empty = jnp.zeros((K,) + spectra.shape, jnp.bfloat16)
    carry = (jnp.int32(0), spectra, high0, empty)
    moved = lax.while_loop(lambda c: c[0] < steps, advance, carry)[3]
    cos_w, sin_w = phase_tables(groups)
    corr = lag_terms(own_re, own_im, moved, cos_w, sin_w)
    summed = lax.psum_scatter(corr, "win", scatter_dimension=0, tiled=True)
    valid = me + offsets < n_chan
    return jnp.where(valid[None, :, None, None], summed, 0.0)


def solution(mesh):
    in_specs = (P("chan", "win"), P(), P("win"))
    out_specs = P("win", None, "chan", None)
    return jax.shard_map(
        on_device, mesh=mesh, in_specs=in_specs, out_specs=out_specs, check_vma=False
    )
```

```python
import math

import jax
import jax.numpy as jnp
import ml_dtypes
import numpy as np
from jax import lax
from jax.sharding import PartitionSpec as P

WIN = 2048
NBIN = 1024
BAND = 64
L = 16
K = 4
OFFCAP = 16


turn_full = 2.0 * math.pi


def dft_table():
    samples = np.arange(WIN, dtype=np.int64)
    bins = np.arange(NBIN, dtype=np.int64)
    turns = samples[:, None] * bins[None, :] % WIN
    angles = np.float32(turn_full / WIN) * turns.astype(np.float32)
    table = np.concatenate([np.cos(angles), -np.sin(angles)], axis=1)
    return jnp.asarray(table.astype(ml_dtypes.bfloat16))


def taper_weights():
    samples = jnp.arange(WIN, dtype=jnp.float32)
    return 0.5 - 0.5 * jnp.cos(turn_full / WIN * (samples + 0.5))


def band_matrix():
    bins = jnp.arange(NBIN, dtype=jnp.int32)
    near = (jnp.abs(bins[:, None] - bins[None, :]) <= BAND).astype(jnp.float32)
    return near / jnp.sum(near, axis=0, keepdims=True)


def phase_tables(windows_total):
    lags = jnp.arange(L, dtype=jnp.int32) - L // 2
    bins = jnp.arange(NBIN, dtype=jnp.int32)
    turns = bins[None, :] * (lags[:, None] + WIN) % WIN
    angles = turn_full / WIN * turns.astype(jnp.float32)
    weight = jnp.where(bins == 0, 1.0, 2.0).astype(jnp.float32) / (
        2.0 * math.sqrt(NBIN * windows_total)
    )
    return (jnp.cos(angles) * weight[None, :], jnp.sin(angles) * weight[None, :])


def whiten(frames, table, taper, band):
    values = frames.astype(jnp.float32)
    shaped = ((values - jnp.mean(values, axis=1, keepdims=True)) * taper[None, :]).astype(
        jnp.bfloat16
    )
    spec = jnp.dot(shaped, table, preferred_element_type=jnp.float32)
    real = spec[:, :NBIN]
    imag = spec[:, NBIN:]
    level = (
        jnp.dot(jnp.sqrt(real * real + imag * imag), band, precision=lax.Precision.HIGHEST) + 1e-05
    )
    return ((real / level).astype(jnp.bfloat16), (imag / level).astype(jnp.bfloat16))


def lag_terms(own_re, own_im, partner, cos_w, sin_w):
    ar = own_re.astype(jnp.float32)[:, None, :]
    ai = own_im.astype(jnp.float32)[:, None, :]
    first = (ar * cos_w[None] - ai * sin_w[None]).astype(jnp.bfloat16)
    second = (ar * sin_w[None] + ai * cos_w[None]).astype(jnp.bfloat16)
    return jnp.einsum(
        "ctf,kjf->tkcj", first, partner[:, 0], preferred_element_type=jnp.float32
    ) + jnp.einsum("ctf,kjf->tkcj", second, partner[:, 1], preferred_element_type=jnp.float32)


def in_blocks(array, dim, size):
    before, after = (array.shape[:dim], array.shape[dim + 1 :])
    return jnp.moveaxis(array.reshape(*before, size, -1, *after), dim, 0)


def on_device(records, offsets, starts):
    n_chan = lax.axis_size("chan")
    groups = lax.axis_size("win")
    me = lax.axis_index("chan")
    frames = lax.dynamic_slice_in_dim(records, starts[0], WIN, 1)
    own_re, own_im = whiten(frames, dft_table(), taper_weights(), band_matrix())
    spectra = jnp.stack((own_re, own_im), axis=0)

    def shifted(by):
        pairs = [(i + by, i) for i in range(n_chan - by)]
        return lambda x: lax.ppermute(x, "chan", pairs)

    branches = [shifted(by) for by in range(1, OFFCAP)]
    moved = jnp.stack(
        [lax.switch(offsets[k] - 1, branches, spectra) for k in range(K)], axis=0
    )
    cos_w, sin_w = phase_tables(groups)
    corr = lag_terms(own_re, own_im, moved, cos_w, sin_w)
    pieces = in_blocks(corr, 0, groups).astype(jnp.bfloat16)
    arrived = lax.all_to_all(pieces, "win", split_axis=0, concat_axis=0, tiled=True)
    return arrived.astype(jnp.float32).sum(axis=0)


def solution(mesh):
    in_specs = (P("chan", "win"), P(), P("win"))
    out_specs = P("win", None, "chan", None)
    return jax.shard_map(
        on_device, mesh=mesh, in_specs=in_specs, out_specs=out_specs, check_vma=False
    )
```

```python
import math

import jax
import jax.numpy as jnp
import ml_dtypes
import numpy as np
from jax import lax
from jax.sharding import PartitionSpec as P

WIN = 2048
NBIN = 1024
BAND = 64
L = 16
K = 4
OFFCAP = 16


turn_full = 2.0 * math.pi


def dft_table():
    samples = np.arange(WIN, dtype=np.int64)
    bins = np.arange(NBIN, dtype=np.int64)
    turns = samples[:, None] * bins[None, :] % WIN
    angles = np.float32(turn_full / WIN) * turns.astype(np.float32)
    table = np.concatenate([np.cos(angles), -np.sin(angles)], axis=1)
    return jnp.asarray(table.astype(ml_dtypes.bfloat16))


def taper_weights():
    samples = jnp.arange(WIN, dtype=jnp.float32)
    return 0.5 - 0.5 * jnp.cos(turn_full / WIN * (samples + 0.5))


def band_matrix():
    bins = jnp.arange(NBIN, dtype=jnp.int32)
    near = (jnp.abs(bins[:, None] - bins[None, :]) <= BAND).astype(jnp.float32)
    return near / jnp.sum(near, axis=0, keepdims=True)


def phase_tables(windows_total):
    lags = jnp.arange(L, dtype=jnp.int32) - L // 2
    bins = jnp.arange(NBIN, dtype=jnp.int32)
    turns = bins[None, :] * (lags[:, None] + WIN) % WIN
    angles = turn_full / WIN * turns.astype(jnp.float32)
    weight = jnp.where(bins == 0, 1.0, 2.0).astype(jnp.float32) / (
        2.0 * math.sqrt(NBIN * windows_total)
    )
    return (jnp.cos(angles) * weight[None, :], jnp.sin(angles) * weight[None, :])


def whiten(frames, table, taper, band):
    values = frames.astype(jnp.float32)
    shaped = ((values - jnp.mean(values, axis=1, keepdims=True)) * taper[None, :]).astype(
        jnp.bfloat16
    )
    spec = jnp.dot(shaped, table, preferred_element_type=jnp.float32)
    real = spec[:, :NBIN]
    imag = spec[:, NBIN:]
    level = (
        jnp.dot(jnp.sqrt(real * real + imag * imag), band, precision=lax.Precision.HIGHEST) + 1e-05
    )
    return ((real / level).astype(jnp.bfloat16), (imag / level).astype(jnp.bfloat16))


def lag_terms(own_re, own_im, partner, cos_w, sin_w):
    ar = own_re.astype(jnp.float32)[:, None, :]
    ai = own_im.astype(jnp.float32)[:, None, :]
    first = (ar * cos_w[None] - ai * sin_w[None]).astype(jnp.bfloat16)
    second = (ar * sin_w[None] + ai * cos_w[None]).astype(jnp.bfloat16)
    return jnp.einsum(
        "ctf,kjf->tkcj", first, partner[:, 0], preferred_element_type=jnp.float32
    ) + jnp.einsum("ctf,kjf->tkcj", second, partner[:, 1], preferred_element_type=jnp.float32)


def in_blocks(array, dim, size):
    before, after = (array.shape[:dim], array.shape[dim + 1 :])
    return jnp.moveaxis(array.reshape(*before, size, -1, *after), dim, 0)


def on_device(records, offsets, starts):
    n_chan = lax.axis_size("chan")
    groups = lax.axis_size("win")
    me = lax.axis_index("chan")
    frames = lax.dynamic_slice_in_dim(records, starts[0], WIN, 1)
    own_re, own_im = whiten(frames, dft_table(), taper_weights(), band_matrix())
    spectra = jnp.stack((own_re, own_im), axis=0)

    def shifted(by):
        pairs = [(i + by, i) for i in range(n_chan - by)]
        return lambda x: lax.ppermute(x, "chan", pairs)

    far = OFFCAP - 1
    farthest = shifted(far)(spectra)
    branches = [shifted(by) for by in range(1, far)] + [jnp.zeros_like]
    moved = jnp.stack(
        [
            jnp.where(offsets[k] == far, farthest, lax.switch(offsets[k] - 1, branches, spectra))
            for k in range(K)
        ],
        axis=0,
    )
    cos_w, sin_w = phase_tables(groups)
    corr = lag_terms(own_re, own_im, moved, cos_w, sin_w)
    pieces = in_blocks(corr, 0, groups).astype(jnp.bfloat16)
    arrived = lax.all_to_all(pieces, "win", split_axis=0, concat_axis=0, tiled=True)
    return arrived.astype(jnp.float32).sum(axis=0)


def solution(mesh):
    in_specs = (P("chan", "win"), P(), P("win"))
    out_specs = P("win", None, "chan", None)
    return jax.shard_map(
        on_device, mesh=mesh, in_specs=in_specs, out_specs=out_specs, check_vma=False
    )
```

```python
import math

import jax
import jax.numpy as jnp
import ml_dtypes
import numpy as np
from jax import lax
from jax.sharding import PartitionSpec as P

WIN = 2048
NBIN = 1024
BAND = 64
L = 16
K = 4
OFFCAP = 16


turn_full = 2.0 * math.pi


def dft_table():
    samples = np.arange(WIN, dtype=np.int64)
    bins = np.arange(NBIN, dtype=np.int64)
    turns = samples[:, None] * bins[None, :] % WIN
    angles = np.float32(turn_full / WIN) * turns.astype(np.float32)
    table = np.concatenate([np.cos(angles), -np.sin(angles)], axis=1)
    return jnp.asarray(table.astype(ml_dtypes.bfloat16))


def taper_weights():
    samples = jnp.arange(WIN, dtype=jnp.float32)
    return 0.5 - 0.5 * jnp.cos(turn_full / WIN * (samples + 0.5))


def band_matrix():
    bins = jnp.arange(NBIN, dtype=jnp.int32)
    near = (jnp.abs(bins[:, None] - bins[None, :]) <= BAND).astype(jnp.float32)
    return near / jnp.sum(near, axis=0, keepdims=True)


def phase_tables(windows_total):
    lags = jnp.arange(L, dtype=jnp.int32) - L // 2
    bins = jnp.arange(NBIN, dtype=jnp.int32)
    turns = bins[None, :] * (lags[:, None] + WIN) % WIN
    angles = turn_full / WIN * turns.astype(jnp.float32)
    weight = jnp.where(bins == 0, 1.0, 2.0).astype(jnp.float32) / (
        2.0 * math.sqrt(NBIN * windows_total)
    )
    return (jnp.cos(angles) * weight[None, :], jnp.sin(angles) * weight[None, :])


def whiten(frames, table, taper, band):
    values = frames.astype(jnp.float32)
    shaped = ((values - jnp.mean(values, axis=1, keepdims=True)) * taper[None, :]).astype(
        jnp.bfloat16
    )
    spec = jnp.dot(shaped, table, preferred_element_type=jnp.float32)
    real = spec[:, :NBIN]
    imag = spec[:, NBIN:]
    level = (
        jnp.dot(jnp.sqrt(real * real + imag * imag), band, precision=lax.Precision.HIGHEST) + 1e-05
    )
    return ((real / level).astype(jnp.bfloat16), (imag / level).astype(jnp.bfloat16))


def lag_factors(own_re, own_im, cos_w, sin_w):
    ar = own_re.astype(jnp.float32)[:, None, :]
    ai = own_im.astype(jnp.float32)[:, None, :]
    first = (ar * cos_w[None] - ai * sin_w[None]).astype(jnp.bfloat16)
    second = (ar * sin_w[None] + ai * cos_w[None]).astype(jnp.bfloat16)
    return first, second


def lag_terms(first, second, partner):
    return jnp.einsum(
        "ctf,jf->tcj", first, partner[0], preferred_element_type=jnp.float32
    ) + jnp.einsum("ctf,jf->tcj", second, partner[1], preferred_element_type=jnp.float32)


def split_for_win(corr):
    groups = lax.axis_size("win")
    me = lax.axis_index("win")
    pieces = corr.reshape(groups, -1, *corr.shape[1:])
    own = lax.dynamic_index_in_dim(pieces, me, 0, keepdims=False)
    sent = [
        lax.dynamic_index_in_dim(pieces, (me + by) % groups, 0, keepdims=False).astype(jnp.bfloat16)
        for by in range(1, groups)
    ]
    return own, sent


def pass_over_win(sent):
    groups = lax.axis_size("win")
    return [
        lax.ppermute(piece, "win", [(w, (w + by) % groups) for w in range(groups)])
        for by, piece in enumerate(sent, start=1)
    ]


def sum_over_win(own, arrived):
    total = own
    for piece in arrived:
        total = total + piece.astype(jnp.float32)
    return total


def in_blocks(array, dim, size):
    before, after = (array.shape[:dim], array.shape[dim + 1 :])
    return jnp.moveaxis(array.reshape(*before, size, -1, *after), dim, 0)


def on_device(records, offsets, starts):
    n_chan = lax.axis_size("chan")
    groups = lax.axis_size("win")
    me = lax.axis_index("chan")
    frames = lax.dynamic_slice_in_dim(records, starts[0], WIN, 1)
    own_re, own_im = whiten(frames, dft_table(), taper_weights(), band_matrix())
    spectra = jnp.stack((own_re, own_im), axis=0)

    def shifted(by):
        pairs = [(i + by, i) for i in range(n_chan - by)]
        return lambda x: lax.ppermute(x, "chan", pairs)

    def with_win(move):
        return lambda x, sent: (move(x), pass_over_win(sent))

    far = OFFCAP - 1
    farthest = shifted(far)(spectra)
    moves = [shifted(by) for by in range(1, far)] + [jnp.zeros_like]
    paired = [with_win(move) for move in moves]
    cos_w, sin_w = phase_tables(groups)
    first, second = lag_factors(own_re, own_im, cos_w, sin_w)
    parts = []
    pending = None
    for k in range(K):
        if pending is None:
            moved = lax.switch(offsets[k] - 1, moves, spectra)
        else:
            moved, arrived = lax.switch(offsets[k] - 1, paired, spectra, pending[1])
            parts.append(sum_over_win(pending[0], arrived))
        partner = jnp.where(offsets[k] == far, farthest, moved)
        pending = split_for_win(lag_terms(first, second, partner))
    parts.append(sum_over_win(pending[0], pass_over_win(pending[1])))
    return jnp.stack(parts, axis=1)


def solution(mesh):
    in_specs = (P("chan", "win"), P(), P("win"))
    out_specs = P("win", None, "chan", None)
    return jax.shard_map(
        on_device, mesh=mesh, in_specs=in_specs, out_specs=out_specs, check_vma=False
    )
```

```python
import math

import jax
import jax.numpy as jnp
import ml_dtypes
import numpy as np
from jax import lax
from jax.sharding import PartitionSpec as P

WIN = 2048
NBIN = 1024
BAND = 64
L = 16
K = 4
OFFCAP = 16


turn_full = 2.0 * math.pi


def dft_table():
    samples = np.arange(WIN, dtype=np.int64)
    bins = np.arange(NBIN, dtype=np.int64)
    turns = samples[:, None] * bins[None, :] % WIN
    angles = np.float32(turn_full / WIN) * turns.astype(np.float32)
    table = np.concatenate([np.cos(angles), -np.sin(angles)], axis=1)
    return jnp.asarray(table.astype(ml_dtypes.bfloat16))


def taper_weights():
    samples = jnp.arange(WIN, dtype=jnp.float32)
    return 0.5 - 0.5 * jnp.cos(turn_full / WIN * (samples + 0.5))


def band_matrix():
    bins = jnp.arange(NBIN, dtype=jnp.int32)
    near = (jnp.abs(bins[:, None] - bins[None, :]) <= BAND).astype(jnp.float32)
    return near / jnp.sum(near, axis=0, keepdims=True)


def phase_tables(windows_total):
    lags = jnp.arange(L, dtype=jnp.int32) - L // 2
    bins = jnp.arange(NBIN, dtype=jnp.int32)
    turns = bins[None, :] * (lags[:, None] + WIN) % WIN
    angles = turn_full / WIN * turns.astype(jnp.float32)
    weight = jnp.where(bins == 0, 1.0, 2.0).astype(jnp.float32) / (
        2.0 * math.sqrt(NBIN * windows_total)
    )
    return (jnp.cos(angles) * weight[None, :], jnp.sin(angles) * weight[None, :])


def whiten(frames, table, taper, band):
    values = frames.astype(jnp.float32)
    shaped = ((values - jnp.mean(values, axis=1, keepdims=True)) * taper[None, :]).astype(
        jnp.bfloat16
    )
    spec = jnp.dot(shaped, table, preferred_element_type=jnp.float32)
    real = spec[:, :NBIN]
    imag = spec[:, NBIN:]
    level = (
        jnp.dot(jnp.sqrt(real * real + imag * imag), band, precision=lax.Precision.HIGHEST) + 1e-05
    )
    return ((real / level).astype(jnp.bfloat16), (imag / level).astype(jnp.bfloat16))


def lag_factors(own_re, own_im, cos_w, sin_w):
    ar = own_re.astype(jnp.float32)[:, None, :]
    ai = own_im.astype(jnp.float32)[:, None, :]
    first = (ar * cos_w[None] - ai * sin_w[None]).astype(jnp.bfloat16)
    second = (ar * sin_w[None] + ai * cos_w[None]).astype(jnp.bfloat16)
    return first, second


def lag_terms(first, second, partner):
    return jnp.einsum(
        "ctf,kjf->tkcj", first, partner[:, 0], preferred_element_type=jnp.float32
    ) + jnp.einsum("ctf,kjf->tkcj", second, partner[:, 1], preferred_element_type=jnp.float32)


def split_for_win(corr):
    groups = lax.axis_size("win")
    me = lax.axis_index("win")
    pieces = corr.reshape(groups, -1, *corr.shape[1:])
    own = lax.dynamic_index_in_dim(pieces, me, 0, keepdims=False)
    sent = [
        lax.dynamic_index_in_dim(pieces, (me + by) % groups, 0, keepdims=False).astype(jnp.bfloat16)
        for by in range(1, groups)
    ]
    return own, sent


def pass_over_win(sent):
    groups = lax.axis_size("win")
    return [
        lax.ppermute(piece, "win", [(w, (w + by) % groups) for w in range(groups)])
        for by, piece in enumerate(sent, start=1)
    ]


def sum_over_win(own, arrived):
    total = own
    for piece in arrived:
        total = total + piece.astype(jnp.float32)
    return total


def in_blocks(array, dim, size):
    before, after = (array.shape[:dim], array.shape[dim + 1 :])
    return jnp.moveaxis(array.reshape(*before, size, -1, *after), dim, 0)


def on_device(records, offsets, starts):
    n_chan = lax.axis_size("chan")
    groups = lax.axis_size("win")
    me = lax.axis_index("chan")
    frames = lax.dynamic_slice_in_dim(records, starts[0], WIN, 1)
    own_re, own_im = whiten(frames, dft_table(), taper_weights(), band_matrix())
    spectra = jnp.stack((own_re, own_im), axis=0)

    def shifted(by):
        pairs = [(i + by, i) for i in range(n_chan - by)]
        return lambda x: lax.ppermute(x, "chan", pairs)

    far = OFFCAP - 1
    farthest = shifted(far)(spectra)
    moves = [shifted(by) for by in range(1, far)] + [jnp.zeros_like]
    cos_w, sin_w = phase_tables(groups)
    first, second = lag_factors(own_re, own_im, cos_w, sin_w)

    def fetched(k, moved):
        return jnp.where(offsets[k] == far, farthest, moved)

    early = jnp.stack(
        [fetched(k, lax.switch(offsets[k] - 1, moves, spectra)) for k in range(K - 1)], axis=0
    )

    early_own, early_sent = split_for_win(lag_terms(first, second, early))

    def with_early(move):
        return lambda x, sent: (move(x), pass_over_win(sent))

    last, early_arrived = lax.switch(
        offsets[K - 1] - 1, [with_early(move) for move in moves], spectra, early_sent
    )
    last_own, last_sent = split_for_win(lag_terms(first, second, fetched(K - 1, last)[None]))
    early_sum = sum_over_win(early_own, early_arrived)
    last_sum = sum_over_win(last_own, pass_over_win(last_sent))
    return jnp.concatenate([early_sum, last_sum], axis=1)


def solution(mesh):
    in_specs = (P("chan", "win"), P(), P("win"))
    out_specs = P("win", None, "chan", None)
    return jax.shard_map(
        on_device, mesh=mesh, in_specs=in_specs, out_specs=out_specs, check_vma=False
    )
```

```python
import math

import jax
import jax.numpy as jnp
import ml_dtypes
import numpy as np
from jax import lax
from jax.sharding import PartitionSpec as P

WIN = 2048
NBIN = 1024
BAND = 64
L = 16
K = 4
OFFCAP = 16


turn_full = 2.0 * math.pi


def dft_table():
    samples = np.arange(WIN, dtype=np.int64)
    bins = np.arange(NBIN, dtype=np.int64)
    turns = samples[:, None] * bins[None, :] % WIN
    angles = np.float32(turn_full / WIN) * turns.astype(np.float32)
    table = np.concatenate([np.cos(angles), -np.sin(angles)], axis=1)
    return jnp.asarray(table.astype(ml_dtypes.bfloat16))


def taper_weights():
    samples = jnp.arange(WIN, dtype=jnp.float32)
    return 0.5 - 0.5 * jnp.cos(turn_full / WIN * (samples + 0.5))


def band_matrix():
    bins = jnp.arange(NBIN, dtype=jnp.int32)
    near = (jnp.abs(bins[:, None] - bins[None, :]) <= BAND).astype(jnp.float32)
    return near / jnp.sum(near, axis=0, keepdims=True)


def phase_tables(windows_total):
    lags = jnp.arange(L, dtype=jnp.int32) - L // 2
    bins = jnp.arange(NBIN, dtype=jnp.int32)
    turns = bins[None, :] * (lags[:, None] + WIN) % WIN
    angles = turn_full / WIN * turns.astype(jnp.float32)
    weight = jnp.where(bins == 0, 1.0, 2.0).astype(jnp.float32) / (
        2.0 * math.sqrt(NBIN * windows_total)
    )
    return (jnp.cos(angles) * weight[None, :], jnp.sin(angles) * weight[None, :])


def whiten(frames, table, taper, band):
    values = frames.astype(jnp.float32)
    shaped = ((values - jnp.mean(values, axis=1, keepdims=True)) * taper[None, :]).astype(
        jnp.bfloat16
    )
    spec = jnp.dot(shaped, table, preferred_element_type=jnp.float32)
    real = spec[:, :NBIN]
    imag = spec[:, NBIN:]
    level = (
        jnp.dot(jnp.sqrt(real * real + imag * imag), band, precision=lax.Precision.HIGHEST) + 1e-05
    )
    return ((real / level).astype(jnp.bfloat16), (imag / level).astype(jnp.bfloat16))


def lag_factors(own_re, own_im, cos_w, sin_w):
    ar = own_re.astype(jnp.float32)[:, None, :]
    ai = own_im.astype(jnp.float32)[:, None, :]
    first = (ar * cos_w[None] - ai * sin_w[None]).astype(jnp.bfloat16)
    second = (ar * sin_w[None] + ai * cos_w[None]).astype(jnp.bfloat16)
    return first, second


def lag_terms(first, second, partner):
    return jnp.einsum(
        "ctf,kjf->tkcj", first, partner[:, 0], preferred_element_type=jnp.float32
    ) + jnp.einsum("ctf,kjf->tkcj", second, partner[:, 1], preferred_element_type=jnp.float32)


def split_for_win(corr):
    groups = lax.axis_size("win")
    me = lax.axis_index("win")
    pieces = corr.reshape(groups, -1, *corr.shape[1:])
    own = lax.dynamic_index_in_dim(pieces, me, 0, keepdims=False)
    return own, pieces.astype(jnp.bfloat16)


def pass_over_win(sent):
    return lax.all_to_all(sent, "win", split_axis=0, concat_axis=0, tiled=True)


def sum_over_win(own, arrived):
    groups = lax.axis_size("win")
    me = lax.axis_index("win")
    others = (jnp.arange(groups) != me).astype(jnp.float32)
    weights = others.reshape(groups, *([1] * (arrived.ndim - 1)))
    return own + jnp.sum(arrived.astype(jnp.float32) * weights, axis=0)


def in_blocks(array, dim, size):
    before, after = (array.shape[:dim], array.shape[dim + 1 :])
    return jnp.moveaxis(array.reshape(*before, size, -1, *after), dim, 0)


def on_device(records, offsets, starts):
    n_chan = lax.axis_size("chan")
    groups = lax.axis_size("win")
    me = lax.axis_index("chan")
    frames = lax.dynamic_slice_in_dim(records, starts[0], WIN, 1)
    own_re, own_im = whiten(frames, dft_table(), taper_weights(), band_matrix())
    spectra = jnp.stack((own_re, own_im), axis=0)

    def shifted(by):
        pairs = [(i + by, i) for i in range(n_chan - by)]
        return lambda x: lax.ppermute(x, "chan", pairs)

    far = OFFCAP - 1
    farthest = shifted(far)(spectra)
    moves = [shifted(by) for by in range(1, far)] + [jnp.zeros_like]
    cos_w, sin_w = phase_tables(groups)
    first, second = lag_factors(own_re, own_im, cos_w, sin_w)

    def fetched(k, moved):
        return jnp.where(offsets[k] == far, farthest, moved)

    early = jnp.stack(
        [fetched(k, lax.switch(offsets[k] - 1, moves, spectra)) for k in range(K - 1)], axis=0
    )

    early_own, early_sent = split_for_win(lag_terms(first, second, early))

    def with_early(move):
        return lambda x, sent: (move(x), pass_over_win(sent))

    last, early_arrived = lax.switch(
        offsets[K - 1] - 1, [with_early(move) for move in moves], spectra, early_sent
    )
    last_own, last_sent = split_for_win(lag_terms(first, second, fetched(K - 1, last)[None]))
    early_sum = sum_over_win(early_own, early_arrived)
    last_sum = sum_over_win(last_own, pass_over_win(last_sent))
    return jnp.concatenate([early_sum, last_sum], axis=1)


def solution(mesh):
    in_specs = (P("chan", "win"), P(), P("win"))
    out_specs = P("win", None, "chan", None)
    return jax.shard_map(
        on_device, mesh=mesh, in_specs=in_specs, out_specs=out_specs, check_vma=False
    )
```

```python
import math

import jax
import jax.numpy as jnp
import ml_dtypes
import numpy as np
from jax import lax
from jax.sharding import PartitionSpec as P

WIN = 2048
NBIN = 1024
BAND = 64
L = 16
K = 4
OFFCAP = 16


turn_full = 2.0 * math.pi


def dft_table():
    samples = np.arange(WIN, dtype=np.int64)
    bins = np.arange(NBIN, dtype=np.int64)
    turns = samples[:, None] * bins[None, :] % WIN
    angles = np.float32(turn_full / WIN) * turns.astype(np.float32)
    table = np.concatenate([np.cos(angles), -np.sin(angles)], axis=1)
    return jnp.asarray(table.astype(ml_dtypes.bfloat16))


def taper_weights():
    samples = jnp.arange(WIN, dtype=jnp.float32)
    return 0.5 - 0.5 * jnp.cos(turn_full / WIN * (samples + 0.5))


def band_matrix():
    bins = jnp.arange(NBIN, dtype=jnp.int32)
    near = (jnp.abs(bins[:, None] - bins[None, :]) <= BAND).astype(jnp.float32)
    return near / jnp.sum(near, axis=0, keepdims=True)


def phase_tables(windows_total):
    lags = jnp.arange(L, dtype=jnp.int32) - L // 2
    bins = jnp.arange(NBIN, dtype=jnp.int32)
    turns = bins[None, :] * (lags[:, None] + WIN) % WIN
    angles = turn_full / WIN * turns.astype(jnp.float32)
    weight = jnp.where(bins == 0, 1.0, 2.0).astype(jnp.float32) / (
        2.0 * math.sqrt(NBIN * windows_total)
    )
    return (jnp.cos(angles) * weight[None, :], jnp.sin(angles) * weight[None, :])


def whiten(frames, table, taper, band):
    values = frames.astype(jnp.float32)
    shaped = ((values - jnp.mean(values, axis=1, keepdims=True)) * taper[None, :]).astype(
        jnp.bfloat16
    )
    spec = jnp.dot(shaped, table, preferred_element_type=jnp.float32)
    real = spec[:, :NBIN]
    imag = spec[:, NBIN:]
    level = (
        jnp.dot(jnp.sqrt(real * real + imag * imag), band, precision=lax.Precision.HIGHEST) + 1e-05
    )
    return ((real / level).astype(jnp.bfloat16), (imag / level).astype(jnp.bfloat16))


def lag_factors(own_re, own_im, cos_w, sin_w):
    ar = own_re.astype(jnp.float32)[:, None, :]
    ai = own_im.astype(jnp.float32)[:, None, :]
    first = (ar * cos_w[None] - ai * sin_w[None]).astype(jnp.bfloat16)
    second = (ar * sin_w[None] + ai * cos_w[None]).astype(jnp.bfloat16)
    return first, second


def lag_terms(first, second, partner):
    return jnp.einsum(
        "ctf,kjf->tkcj", first, partner[:, 0], preferred_element_type=jnp.float32
    ) + jnp.einsum("ctf,kjf->tkcj", second, partner[:, 1], preferred_element_type=jnp.float32)


def split_for_win(corr):
    groups = lax.axis_size("win")
    me = lax.axis_index("win")
    pieces = corr.reshape(groups, -1, *corr.shape[1:])
    own = lax.dynamic_index_in_dim(pieces, me, 0, keepdims=False)
    return own, pieces.astype(jnp.bfloat16)


def pass_over_win(sent):
    return lax.all_to_all(sent, "win", split_axis=0, concat_axis=0, tiled=True)


def sum_over_win(own, arrived):
    groups = lax.axis_size("win")
    me = lax.axis_index("win")
    others = (jnp.arange(groups) != me).astype(jnp.float32)
    weights = others.reshape(groups, *([1] * (arrived.ndim - 1)))
    return own + jnp.sum(arrived.astype(jnp.float32) * weights, axis=0)


def in_blocks(array, dim, size):
    before, after = (array.shape[:dim], array.shape[dim + 1 :])
    return jnp.moveaxis(array.reshape(*before, size, -1, *after), dim, 0)


def on_device(records, offsets, starts):
    n_chan = lax.axis_size("chan")
    groups = lax.axis_size("win")
    me = lax.axis_index("chan")
    frames = lax.dynamic_slice_in_dim(records, starts[0], WIN, 1)
    own_re, own_im = whiten(frames, dft_table(), taper_weights(), band_matrix())
    spectra = jnp.stack((own_re, own_im), axis=0)

    def shifted(by):
        pairs = [(i + by, i) for i in range(n_chan - by)]
        return lambda x: lax.ppermute(x, "chan", pairs)

    far = OFFCAP - 1
    farthest = shifted(far)(spectra)
    moves = [shifted(by) for by in range(1, far)]
    cos_w, sin_w = phase_tables(groups)
    first, second = lag_factors(own_re, own_im, cos_w, sin_w)
    order = jnp.sort(offsets)
    rank = jnp.sum(offsets[None, :] < offsets[:, None], axis=1)
    nearer = [lax.switch(order[k] - 1, moves, spectra) for k in range(K - 2)]
    early = jnp.stack([farthest] + nearer, axis=0)
    early_own, early_sent = split_for_win(lag_terms(first, second, early))

    def with_early(move):
        return lambda x, sent: (move(x), pass_over_win(sent))

    last, early_arrived = lax.switch(
        order[K - 2] - 1, [with_early(move) for move in moves], spectra, early_sent
    )
    last_own, last_sent = split_for_win(lag_terms(first, second, last[None]))
    early_sum = sum_over_win(early_own, early_arrived)
    last_sum = sum_over_win(last_own, pass_over_win(last_sent))
    by_rank = jnp.concatenate([early_sum[:, 1:], last_sum, early_sum[:, :1]], axis=1)
    return jnp.take(by_rank, rank, axis=1)


def solution(mesh):
    in_specs = (P("chan", "win"), P(), P("win"))
    out_specs = P("win", None, "chan", None)
    return jax.shard_map(
        on_device, mesh=mesh, in_specs=in_specs, out_specs=out_specs, check_vma=False
    )
```

```python
import math

import jax
import jax.numpy as jnp
import ml_dtypes
import numpy as np
from jax import lax
from jax.sharding import PartitionSpec as P

WIN = 2048
NBIN = 1024
BAND = 64
L = 16
K = 4
OFFCAP = 16


turn_full = 2.0 * math.pi


def dft_table():
    samples = np.arange(WIN, dtype=np.int64)
    bins = np.arange(NBIN, dtype=np.int64)
    turns = samples[:, None] * bins[None, :] % WIN
    angles = np.float32(turn_full / WIN) * turns.astype(np.float32)
    table = np.concatenate([np.cos(angles), -np.sin(angles)], axis=1)
    return jnp.asarray(table.astype(ml_dtypes.bfloat16))


def taper_weights():
    samples = jnp.arange(WIN, dtype=jnp.float32)
    return 0.5 - 0.5 * jnp.cos(turn_full / WIN * (samples + 0.5))


def band_matrix():
    bins = jnp.arange(NBIN, dtype=jnp.int32)
    near = (jnp.abs(bins[:, None] - bins[None, :]) <= BAND).astype(jnp.float32)
    return near / jnp.sum(near, axis=0, keepdims=True)


def phase_tables(windows_total):
    lags = jnp.arange(L, dtype=jnp.int32) - L // 2
    bins = jnp.arange(NBIN, dtype=jnp.int32)
    turns = bins[None, :] * (lags[:, None] + WIN) % WIN
    angles = turn_full / WIN * turns.astype(jnp.float32)
    weight = jnp.where(bins == 0, 1.0, 2.0).astype(jnp.float32) / (
        2.0 * math.sqrt(NBIN * windows_total)
    )
    return (jnp.cos(angles) * weight[None, :], jnp.sin(angles) * weight[None, :])


def whiten(frames, table, taper, band):
    values = frames.astype(jnp.float32)
    shaped = ((values - jnp.mean(values, axis=1, keepdims=True)) * taper[None, :]).astype(
        jnp.bfloat16
    )
    spec = jnp.dot(shaped, table, preferred_element_type=jnp.float32)
    real = spec[:, :NBIN]
    imag = spec[:, NBIN:]
    level = (
        jnp.dot(jnp.sqrt(real * real + imag * imag), band, precision=lax.Precision.HIGHEST) + 1e-05
    )
    return ((real / level).astype(jnp.bfloat16), (imag / level).astype(jnp.bfloat16))


def lag_factors(own_re, own_im, cos_w, sin_w):
    ar = own_re.astype(jnp.float32)[:, None, :]
    ai = own_im.astype(jnp.float32)[:, None, :]
    first = (ar * cos_w[None] - ai * sin_w[None]).astype(jnp.bfloat16)
    second = (ar * sin_w[None] + ai * cos_w[None]).astype(jnp.bfloat16)
    return first, second


def lag_terms(first, second, partner):
    return jnp.einsum(
        "ctf,kjf->tkcj", first, partner[:, 0], preferred_element_type=jnp.float32
    ) + jnp.einsum("ctf,kjf->tkcj", second, partner[:, 1], preferred_element_type=jnp.float32)


def split_for_win(corr):
    groups = lax.axis_size("win")
    me = lax.axis_index("win")
    pieces = corr.reshape(groups, -1, *corr.shape[1:])
    own = lax.dynamic_index_in_dim(pieces, me, 0, keepdims=False)
    return own, pieces.astype(jnp.bfloat16)


def pass_over_win(sent):
    return lax.all_to_all(sent, "win", split_axis=0, concat_axis=0, tiled=True)


def sum_over_win(own, arrived):
    groups = lax.axis_size("win")
    me = lax.axis_index("win")
    others = (jnp.arange(groups) != me).astype(jnp.float32)
    weights = others.reshape(groups, *([1] * (arrived.ndim - 1)))
    return own + jnp.sum(arrived.astype(jnp.float32) * weights, axis=0)


def in_blocks(array, dim, size):
    before, after = (array.shape[:dim], array.shape[dim + 1 :])
    return jnp.moveaxis(array.reshape(*before, size, -1, *after), dim, 0)


def on_device(records, offsets, starts):
    n_chan = lax.axis_size("chan")
    groups = lax.axis_size("win")
    me = lax.axis_index("chan")
    frames = lax.dynamic_slice_in_dim(records, starts[0], WIN, 1)
    own_re, own_im = whiten(frames, dft_table(), taper_weights(), band_matrix())
    spectra = jnp.stack((own_re, own_im), axis=0)

    def shifted(by):
        pairs = [(i + by, i) for i in range(n_chan - by)]
        return lambda x: lax.ppermute(x, "chan", pairs)

    far = OFFCAP - 1
    farthest = shifted(far)(spectra)
    moves = [shifted(by) for by in range(1, far)]
    cos_w, sin_w = phase_tables(groups)
    first, second = lag_factors(own_re, own_im, cos_w, sin_w)
    order = jnp.sort(offsets)
    rank = jnp.sum(offsets[None, :] < offsets[:, None], axis=1)
    pairs_of = [(a, b) for a in range(1, far) for b in range(a + 1, far)]
    pair_index = np.zeros((OFFCAP, OFFCAP), np.int32)
    for index, (a, b) in enumerate(pairs_of):
        pair_index[a, b] = index

    def both(a, b):
        return lambda x: (shifted(a)(x), shifted(b)(x))

    nearer = lax.switch(
        jnp.asarray(pair_index)[order[0], order[2]], [both(a, b) for a, b in pairs_of], spectra
    )
    early = jnp.stack([farthest, nearer[0], nearer[1]], axis=0)
    early_own, early_sent = split_for_win(lag_terms(first, second, early))

    def with_early(move):
        return lambda x, sent: (move(x), pass_over_win(sent))

    last, early_arrived = lax.switch(
        order[1] - 1, [with_early(move) for move in moves], spectra, early_sent
    )
    last_own, last_sent = split_for_win(lag_terms(first, second, last[None]))
    early_sum = sum_over_win(early_own, early_arrived)
    last_sum = sum_over_win(last_own, pass_over_win(last_sent))
    by_rank = jnp.concatenate(
        [early_sum[:, 1:2], last_sum, early_sum[:, 2:3], early_sum[:, :1]], axis=1
    )
    return jnp.take(by_rank, rank, axis=1)


def solution(mesh):
    in_specs = (P("chan", "win"), P(), P("win"))
    out_specs = P("win", None, "chan", None)
    return jax.shard_map(
        on_device, mesh=mesh, in_specs=in_specs, out_specs=out_specs, check_vma=False
    )
```

```python
import math

import jax
import jax.numpy as jnp
import ml_dtypes
import numpy as np
from jax import lax
from jax.sharding import PartitionSpec as P

WIN = 2048
NBIN = 1024
BAND = 64
L = 16
K = 4
OFFCAP = 16


turn_full = 2.0 * math.pi


def dft_table():
    samples = np.arange(WIN, dtype=np.int64)
    bins = np.arange(NBIN, dtype=np.int64)
    turns = samples[:, None] * bins[None, :] % WIN
    angles = np.float32(turn_full / WIN) * turns.astype(np.float32)
    table = np.concatenate([np.cos(angles), -np.sin(angles)], axis=1)
    return jnp.asarray(table.astype(ml_dtypes.bfloat16))


def taper_weights():
    samples = jnp.arange(WIN, dtype=jnp.float32)
    return 0.5 - 0.5 * jnp.cos(turn_full / WIN * (samples + 0.5))


def band_matrix():
    bins = jnp.arange(NBIN, dtype=jnp.int32)
    near = (jnp.abs(bins[:, None] - bins[None, :]) <= BAND).astype(jnp.float32)
    return near / jnp.sum(near, axis=0, keepdims=True)


def phase_tables(windows_total):
    lags = jnp.arange(L, dtype=jnp.int32) - L // 2
    bins = jnp.arange(NBIN, dtype=jnp.int32)
    turns = bins[None, :] * (lags[:, None] + WIN) % WIN
    angles = turn_full / WIN * turns.astype(jnp.float32)
    weight = jnp.where(bins == 0, 1.0, 2.0).astype(jnp.float32) / (
        2.0 * math.sqrt(NBIN * windows_total)
    )
    return (jnp.cos(angles) * weight[None, :], jnp.sin(angles) * weight[None, :])


def whiten(frames, table, taper, band):
    values = frames.astype(jnp.float32)
    shaped = ((values - jnp.mean(values, axis=1, keepdims=True)) * taper[None, :]).astype(
        jnp.bfloat16
    )
    spec = jnp.dot(shaped, table, preferred_element_type=jnp.float32)
    real = spec[:, :NBIN]
    imag = spec[:, NBIN:]
    level = (
        jnp.dot(jnp.sqrt(real * real + imag * imag), band, precision=lax.Precision.HIGHEST) + 1e-05
    )
    return (spec / jnp.concatenate([level, level], axis=1)).astype(jnp.bfloat16)


def lag_factors(white, cos_w, sin_w):
    ar = white[:, None, :NBIN].astype(jnp.float32)
    ai = white[:, None, NBIN:].astype(jnp.float32)
    first = ar * cos_w[None] - ai * sin_w[None]
    second = ar * sin_w[None] + ai * cos_w[None]
    return jnp.concatenate([first, second], axis=2).astype(jnp.bfloat16)


def lag_terms(factors, partner):
    return jnp.einsum("ctf,kjf->tkcj", factors, partner, preferred_element_type=jnp.float32)


def split_for_win(corr):
    groups = lax.axis_size("win")
    me = lax.axis_index("win")
    pieces = corr.reshape(groups, -1, *corr.shape[1:])
    own = lax.dynamic_index_in_dim(pieces, me, 0, keepdims=False)
    return own, pieces.astype(jnp.bfloat16)


def pass_over_win(sent):
    return lax.all_to_all(sent, "win", split_axis=0, concat_axis=0, tiled=True)


def sum_over_win(own, arrived):
    groups = lax.axis_size("win")
    me = lax.axis_index("win")
    others = (jnp.arange(groups) != me).astype(jnp.float32)
    weights = others.reshape(groups, *([1] * (arrived.ndim - 1)))
    return own + jnp.sum(arrived.astype(jnp.float32) * weights, axis=0)


def in_blocks(array, dim, size):
    before, after = (array.shape[:dim], array.shape[dim + 1 :])
    return jnp.moveaxis(array.reshape(*before, size, -1, *after), dim, 0)


def on_device(records, offsets, starts):
    n_chan = lax.axis_size("chan")
    groups = lax.axis_size("win")
    me = lax.axis_index("chan")
    frames = lax.dynamic_slice_in_dim(records, starts[0], WIN, 1)
    spectra = whiten(frames, dft_table(), taper_weights(), band_matrix())

    def shifted(by):
        pairs = [(i + by, i) for i in range(n_chan - by)]
        return lambda x: lax.ppermute(x, "chan", pairs)

    far = OFFCAP - 1
    farthest = shifted(far)(spectra)
    moves = [shifted(by) for by in range(1, far)]
    cos_w, sin_w = phase_tables(groups)
    factors = lag_factors(spectra, cos_w, sin_w)
    order = jnp.sort(offsets)
    rank = jnp.sum(offsets[None, :] < offsets[:, None], axis=1)
    nearer = [lax.switch(order[k] - 1, moves, spectra) for k in range(K - 2)]
    early = jnp.stack([farthest] + nearer, axis=0)
    early_own, early_sent = split_for_win(lag_terms(factors, early))

    def with_early(move):
        return lambda x, sent: (move(x), pass_over_win(sent))

    last, early_arrived = lax.switch(
        order[K - 2] - 1, [with_early(move) for move in moves], spectra, early_sent
    )
    last_own, last_sent = split_for_win(lag_terms(factors, last[None]))
    early_sum = sum_over_win(early_own, early_arrived)
    last_sum = sum_over_win(last_own, pass_over_win(last_sent))
    by_rank = jnp.concatenate([early_sum[:, 1:], last_sum, early_sum[:, :1]], axis=1)
    return jnp.take(by_rank, rank, axis=1)


def solution(mesh):
    in_specs = (P("chan", "win"), P(), P("win"))
    out_specs = P("win", None, "chan", None)
    return jax.shard_map(
        on_device, mesh=mesh, in_specs=in_specs, out_specs=out_specs, check_vma=False
    )
```

```python
import math

import jax
import jax.numpy as jnp
import ml_dtypes
import numpy as np
from jax import lax
from jax.sharding import PartitionSpec as P

WIN = 2048
NBIN = 1024
BAND = 64
L = 16
K = 4
OFFCAP = 16


turn_full = 2.0 * math.pi


def dft_table():
    samples = np.arange(WIN, dtype=np.int64)
    bins = np.arange(NBIN, dtype=np.int64)
    turns = samples[:, None] * bins[None, :] % WIN
    angles = np.float32(turn_full / WIN) * turns.astype(np.float32)
    table = np.concatenate([np.cos(angles), -np.sin(angles)], axis=1)
    return jnp.asarray(table.astype(ml_dtypes.bfloat16))


def taper_weights():
    samples = jnp.arange(WIN, dtype=jnp.float32)
    return 0.5 - 0.5 * jnp.cos(turn_full / WIN * (samples + 0.5))


def band_matrix():
    bins = jnp.arange(NBIN, dtype=jnp.int32)
    near = (jnp.abs(bins[:, None] - bins[None, :]) <= BAND).astype(jnp.float32)
    return near / jnp.sum(near, axis=0, keepdims=True)


def phase_tables(windows_total):
    lags = jnp.arange(L, dtype=jnp.int32) - L // 2
    bins = jnp.arange(NBIN, dtype=jnp.int32)
    turns = bins[None, :] * (lags[:, None] + WIN) % WIN
    angles = turn_full / WIN * turns.astype(jnp.float32)
    weight = jnp.where(bins == 0, 1.0, 2.0).astype(jnp.float32) / (
        2.0 * math.sqrt(NBIN * windows_total)
    )
    return (jnp.cos(angles) * weight[None, :], jnp.sin(angles) * weight[None, :])


def whiten(frames, table, taper, band):
    values = frames.astype(jnp.float32)
    shaped = ((values - jnp.mean(values, axis=1, keepdims=True)) * taper[None, :]).astype(
        jnp.bfloat16
    )
    spec = jnp.dot(shaped, table, preferred_element_type=jnp.float32)
    real = spec[:, :NBIN]
    imag = spec[:, NBIN:]
    level = (
        jnp.dot(jnp.sqrt(real * real + imag * imag), band, precision=lax.Precision.HIGHEST) + 1e-05
    )
    return ((real / level).astype(jnp.bfloat16), (imag / level).astype(jnp.bfloat16))


def lag_factors(own_re, own_im, cos_w, sin_w):
    ar = own_re.astype(jnp.float32)[:, None, :]
    ai = own_im.astype(jnp.float32)[:, None, :]
    first = (ar * cos_w[None] - ai * sin_w[None]).astype(jnp.bfloat16)
    second = (ar * sin_w[None] + ai * cos_w[None]).astype(jnp.bfloat16)
    return first, second


def lag_terms(first, second, partner):
    return jnp.einsum(
        "ctf,kjf->tkcj", first, partner[:, 0], preferred_element_type=jnp.float32
    ) + jnp.einsum("ctf,kjf->tkcj", second, partner[:, 1], preferred_element_type=jnp.float32)


def split_for_win(corr):
    groups = lax.axis_size("win")
    me = lax.axis_index("win")
    pieces = corr.reshape(groups, -1, *corr.shape[1:])
    own = lax.dynamic_index_in_dim(pieces, me, 0, keepdims=False)
    return own, pieces.astype(jnp.bfloat16)


def pass_over_win(sent):
    return lax.all_to_all(sent, "win", split_axis=0, concat_axis=0, tiled=True)


def sum_over_win(own, arrived):
    groups = lax.axis_size("win")
    me = lax.axis_index("win")
    others = (jnp.arange(groups) != me).astype(jnp.float32)
    weights = others.reshape(groups, *([1] * (arrived.ndim - 1)))
    return own + jnp.sum(arrived.astype(jnp.float32) * weights, axis=0)


def in_blocks(array, dim, size):
    before, after = (array.shape[:dim], array.shape[dim + 1 :])
    return jnp.moveaxis(array.reshape(*before, size, -1, *after), dim, 0)


def on_device(records, offsets, starts):
    n_chan = lax.axis_size("chan")
    groups = lax.axis_size("win")
    me = lax.axis_index("chan")
    frames = lax.dynamic_slice_in_dim(records, starts[0], WIN, 1)
    table = dft_table()
    taper = taper_weights()
    band = band_matrix()

    def whitened(x):
        return jnp.stack(whiten(x, table, taper, band), axis=0)

    def shifted(by):
        pairs = [(i + by, i) for i in range(n_chan - by)]
        return lambda x: lax.ppermute(x, "chan", pairs)

    def beside(move):
        return lambda x, y: (move(x), whitened(y))

    far = OFFCAP - 1
    moves = [shifted(by) for by in range(1, far)]
    paired = [beside(move) for move in moves]
    order = jnp.sort(offsets)
    rank = jnp.sum(offsets[None, :] < offsets[:, None], axis=1)
    near_frames, spectra = lax.switch(order[0] - 1, paired, frames, frames)
    own_re, own_im = spectra[0], spectra[1]
    farthest = shifted(far)(spectra)
    second_near, first_near = lax.switch(order[1] - 1, paired, spectra, near_frames)
    nearer = [first_near, second_near]
    cos_w, sin_w = phase_tables(groups)
    first, second = lag_factors(own_re, own_im, cos_w, sin_w)
    early = jnp.stack([farthest] + nearer, axis=0)
    early_own, early_sent = split_for_win(lag_terms(first, second, early))

    def with_early(move):
        return lambda x, sent: (move(x), pass_over_win(sent))

    last, early_arrived = lax.switch(
        order[K - 2] - 1, [with_early(move) for move in moves], spectra, early_sent
    )
    last_own, last_sent = split_for_win(lag_terms(first, second, last[None]))
    early_sum = sum_over_win(early_own, early_arrived)
    last_sum = sum_over_win(last_own, pass_over_win(last_sent))
    by_rank = jnp.concatenate([early_sum[:, 1:], last_sum, early_sum[:, :1]], axis=1)
    return jnp.take(by_rank, rank, axis=1)


def solution(mesh):
    in_specs = (P("chan", "win"), P(), P("win"))
    out_specs = P("win", None, "chan", None)
    return jax.shard_map(
        on_device, mesh=mesh, in_specs=in_specs, out_specs=out_specs, check_vma=False
    )
```

```python
import math

import jax
import jax.numpy as jnp
import ml_dtypes
import numpy as np
from jax import lax
from jax.sharding import PartitionSpec as P

WIN = 2048
NBIN = 1024
BAND = 64
L = 16
K = 4
OFFCAP = 16


turn_full = 2.0 * math.pi


def dft_table():
    samples = np.arange(WIN, dtype=np.int64)
    bins = np.arange(NBIN, dtype=np.int64)
    turns = samples[:, None] * bins[None, :] % WIN
    angles = np.float32(turn_full / WIN) * turns.astype(np.float32)
    table = np.concatenate([np.cos(angles), -np.sin(angles)], axis=1)
    return jnp.asarray(table.astype(ml_dtypes.bfloat16))


def taper_weights():
    samples = jnp.arange(WIN, dtype=jnp.float32)
    return 0.5 - 0.5 * jnp.cos(turn_full / WIN * (samples + 0.5))


def band_matrix():
    bins = jnp.arange(NBIN, dtype=jnp.int32)
    near = (jnp.abs(bins[:, None] - bins[None, :]) <= BAND).astype(jnp.float32)
    return near / jnp.sum(near, axis=0, keepdims=True)


def phase_tables(windows_total):
    lags = jnp.arange(L, dtype=jnp.int32) - L // 2
    bins = jnp.arange(NBIN, dtype=jnp.int32)
    turns = bins[None, :] * (lags[:, None] + WIN) % WIN
    angles = turn_full / WIN * turns.astype(jnp.float32)
    weight = jnp.where(bins == 0, 1.0, 2.0).astype(jnp.float32) / (
        2.0 * math.sqrt(NBIN * windows_total)
    )
    return (jnp.cos(angles) * weight[None, :], jnp.sin(angles) * weight[None, :])


def whiten(frames, table, taper, band):
    values = frames.astype(jnp.float32)
    shaped = ((values - jnp.mean(values, axis=1, keepdims=True)) * taper[None, :]).astype(
        jnp.bfloat16
    )
    spec = jnp.dot(shaped, table, preferred_element_type=jnp.float32)
    real = spec[:, :NBIN]
    imag = spec[:, NBIN:]
    level = (
        jnp.dot(jnp.sqrt(real * real + imag * imag), band, precision=lax.Precision.HIGHEST) + 1e-05
    )
    return ((real / level).astype(jnp.bfloat16), (imag / level).astype(jnp.bfloat16))


def lag_factors(own_re, own_im, cos_w, sin_w):
    ar = own_re.astype(jnp.float32)[:, None, :]
    ai = own_im.astype(jnp.float32)[:, None, :]
    first = (ar * cos_w[None] - ai * sin_w[None]).astype(jnp.bfloat16)
    second = (ar * sin_w[None] + ai * cos_w[None]).astype(jnp.bfloat16)
    return first, second


def lag_terms(first, second, partner):
    return jnp.einsum(
        "ctf,kjf->tkcj", first, partner[:, 0], preferred_element_type=jnp.float32
    ) + jnp.einsum("ctf,kjf->tkcj", second, partner[:, 1], preferred_element_type=jnp.float32)


def split_for_win(corr):
    groups = lax.axis_size("win")
    me = lax.axis_index("win")
    pieces = corr.reshape(groups, -1, *corr.shape[1:])
    own = lax.dynamic_index_in_dim(pieces, me, 0, keepdims=False)
    return own, pieces.astype(jnp.bfloat16)


def pass_over_win(sent):
    return lax.all_to_all(sent, "win", split_axis=0, concat_axis=0, tiled=True)


def sum_over_win(own, arrived):
    groups = lax.axis_size("win")
    me = lax.axis_index("win")
    others = (jnp.arange(groups) != me).astype(jnp.float32)
    weights = others.reshape(groups, *([1] * (arrived.ndim - 1)))
    return own + jnp.sum(arrived.astype(jnp.float32) * weights, axis=0)


def in_blocks(array, dim, size):
    before, after = (array.shape[:dim], array.shape[dim + 1 :])
    return jnp.moveaxis(array.reshape(*before, size, -1, *after), dim, 0)


def on_device(records, offsets, starts):
    n_chan = lax.axis_size("chan")
    groups = lax.axis_size("win")
    me = lax.axis_index("chan")
    frames = lax.dynamic_slice_in_dim(records, starts[0], WIN, 1)
    own_re, own_im = whiten(frames, dft_table(), taper_weights(), band_matrix())
    spectra = jnp.stack((own_re, own_im), axis=0)

    def shifted(by):
        pairs = [(i + by, i) for i in range(n_chan - by)]
        return lambda x: lax.ppermute(x, "chan", pairs)

    far = OFFCAP - 1
    farthest = shifted(far)(spectra)
    moves = [shifted(by) for by in range(1, far)]
    cos_w, sin_w = phase_tables(groups)
    first, second = lag_factors(own_re, own_im, cos_w, sin_w)
    hops = jnp.minimum(offsets, OFFCAP - offsets)
    key = jnp.where(offsets == far, -1, hops * OFFCAP + offsets)
    order = jnp.sort(key)[1:] % OFFCAP
    rank = jnp.sum(key[None, :] < key[:, None], axis=1)
    nearer = [lax.switch(order[k] - 1, moves, spectra) for k in range(K - 2)]
    early = jnp.stack([farthest] + nearer, axis=0)
    early_own, early_sent = split_for_win(lag_terms(first, second, early))

    def with_early(move):
        return lambda x, sent: (move(x), pass_over_win(sent))

    last, early_arrived = lax.switch(
        order[K - 2] - 1, [with_early(move) for move in moves], spectra, early_sent
    )
    last_own, last_sent = split_for_win(lag_terms(first, second, last[None]))
    early_sum = sum_over_win(early_own, early_arrived)
    last_sum = sum_over_win(last_own, pass_over_win(last_sent))
    by_rank = jnp.concatenate([early_sum, last_sum], axis=1)
    return jnp.take(by_rank, rank, axis=1)


def solution(mesh):
    in_specs = (P("chan", "win"), P(), P("win"))
    out_specs = P("win", None, "chan", None)
    return jax.shard_map(
        on_device, mesh=mesh, in_specs=in_specs, out_specs=out_specs, check_vma=False
    )
```

```python
import math

import jax
import jax.numpy as jnp
import ml_dtypes
import numpy as np
from jax import lax
from jax.sharding import PartitionSpec as P

WIN = 2048
NBIN = 1024
BAND = 64
L = 16
K = 4
OFFCAP = 16


turn_full = 2.0 * math.pi


def dft_table():
    samples = np.arange(WIN, dtype=np.int64)
    bins = np.arange(NBIN, dtype=np.int64)
    turns = samples[:, None] * bins[None, :] % WIN
    angles = np.float32(turn_full / WIN) * turns.astype(np.float32)
    table = np.concatenate([np.cos(angles), -np.sin(angles)], axis=1)
    return jnp.asarray(table.astype(ml_dtypes.bfloat16))


def taper_weights():
    samples = jnp.arange(WIN, dtype=jnp.float32)
    return 0.5 - 0.5 * jnp.cos(turn_full / WIN * (samples + 0.5))


def band_matrix():
    bins = jnp.arange(NBIN, dtype=jnp.int32)
    near = (jnp.abs(bins[:, None] - bins[None, :]) <= BAND).astype(jnp.float32)
    return near / jnp.sum(near, axis=0, keepdims=True)


def phase_tables(windows_total):
    lags = jnp.arange(L, dtype=jnp.int32) - L // 2
    bins = jnp.arange(NBIN, dtype=jnp.int32)
    turns = bins[None, :] * (lags[:, None] + WIN) % WIN
    angles = turn_full / WIN * turns.astype(jnp.float32)
    weight = jnp.where(bins == 0, 1.0, 2.0).astype(jnp.float32) / (
        2.0 * math.sqrt(NBIN * windows_total)
    )
    return (jnp.cos(angles) * weight[None, :], jnp.sin(angles) * weight[None, :])


def whiten(frames, table, taper, band):
    values = frames.astype(jnp.float32)
    shaped = ((values - jnp.mean(values, axis=1, keepdims=True)) * taper[None, :]).astype(
        jnp.bfloat16
    )
    spec = jnp.dot(shaped, table, preferred_element_type=jnp.float32)
    real = spec[:, :NBIN]
    imag = spec[:, NBIN:]
    level = (
        jnp.dot(jnp.sqrt(real * real + imag * imag), band, precision=lax.Precision.HIGHEST) + 1e-05
    )
    return ((real / level).astype(jnp.bfloat16), (imag / level).astype(jnp.bfloat16))


def lag_factors(own_re, own_im, cos_w, sin_w):
    ar = own_re.astype(jnp.float32)[:, None, :]
    ai = own_im.astype(jnp.float32)[:, None, :]
    first = (ar * cos_w[None] - ai * sin_w[None]).astype(jnp.bfloat16)
    second = (ar * sin_w[None] + ai * cos_w[None]).astype(jnp.bfloat16)
    return first, second


def lag_terms(first, second, partner):
    return jnp.einsum(
        "ctf,kjf->tkcj", first, partner[:, 0], preferred_element_type=jnp.float32
    ) + jnp.einsum("ctf,kjf->tkcj", second, partner[:, 1], preferred_element_type=jnp.float32)


def split_for_win(corr):
    groups = lax.axis_size("win")
    return corr.reshape(groups, -1, *corr.shape[1:]).astype(jnp.bfloat16)


def pass_over_win(sent):
    return lax.all_to_all(sent, "win", split_axis=0, concat_axis=0, tiled=True)


def sum_over_win(arrived):
    return jnp.sum(arrived.astype(jnp.float32), axis=0)


def in_blocks(array, dim, size):
    before, after = (array.shape[:dim], array.shape[dim + 1 :])
    return jnp.moveaxis(array.reshape(*before, size, -1, *after), dim, 0)


def on_device(records, offsets, starts):
    n_chan = lax.axis_size("chan")
    groups = lax.axis_size("win")
    me = lax.axis_index("chan")
    frames = lax.dynamic_slice_in_dim(records, starts[0], WIN, 1)
    own_re, own_im = whiten(frames, dft_table(), taper_weights(), band_matrix())
    spectra = jnp.stack((own_re, own_im), axis=0)

    def shifted(by):
        pairs = [(i + by, i) for i in range(n_chan - by)]
        return lambda x: lax.ppermute(x, "chan", pairs)

    far = OFFCAP - 1
    farthest = shifted(far)(spectra)
    moves = [shifted(by) for by in range(1, far)]
    cos_w, sin_w = phase_tables(groups)
    first, second = lag_factors(own_re, own_im, cos_w, sin_w)
    hops = jnp.minimum(offsets, OFFCAP - offsets)
    key = jnp.where(offsets == far, -1, hops * OFFCAP + offsets)
    order = jnp.sort(key)[1:] % OFFCAP
    rank = jnp.sum(key[None, :] < key[:, None], axis=1)
    nearer = [lax.switch(order[k] - 1, moves, spectra) for k in range(K - 2)]
    early = jnp.stack([farthest] + nearer, axis=0)
    early_sent = split_for_win(lag_terms(first, second, early))

    def with_early(move):
        return lambda x, sent: (move(x), pass_over_win(sent))

    last, early_arrived = lax.switch(
        order[K - 2] - 1, [with_early(move) for move in moves], spectra, early_sent
    )
    last_sent = split_for_win(lag_terms(first, second, last[None]))
    early_sum = sum_over_win(early_arrived)
    last_sum = sum_over_win(pass_over_win(last_sent))
    by_rank = jnp.concatenate([early_sum, last_sum], axis=1)
    return jnp.take(by_rank, rank, axis=1)


def solution(mesh):
    in_specs = (P("chan", "win"), P(), P("win"))
    out_specs = P("win", None, "chan", None)
    return jax.shard_map(
        on_device, mesh=mesh, in_specs=in_specs, out_specs=out_specs, check_vma=False
    )
```

```python
import math

import jax
import jax.numpy as jnp
import ml_dtypes
import numpy as np
from jax import lax
from jax.sharding import PartitionSpec as P

WIN = 2048
NBIN = 1024
BAND = 64
L = 16
K = 4
OFFCAP = 16


turn_full = 2.0 * math.pi


def dft_table():
    samples = np.arange(WIN, dtype=np.int64)
    bins = np.arange(NBIN, dtype=np.int64)
    turns = samples[:, None] * bins[None, :] % WIN
    angles = np.float32(turn_full / WIN) * turns.astype(np.float32)
    table = np.concatenate([np.cos(angles), -np.sin(angles)], axis=1)
    return jnp.asarray(table.astype(ml_dtypes.bfloat16))


def taper_weights():
    samples = jnp.arange(WIN, dtype=jnp.float32)
    return 0.5 - 0.5 * jnp.cos(turn_full / WIN * (samples + 0.5))


def band_matrix():
    bins = jnp.arange(NBIN, dtype=jnp.int32)
    near = (jnp.abs(bins[:, None] - bins[None, :]) <= BAND).astype(jnp.float32)
    return near / jnp.sum(near, axis=0, keepdims=True)


def phase_tables(windows_total):
    lags = jnp.arange(L, dtype=jnp.int32) - L // 2
    bins = jnp.arange(NBIN, dtype=jnp.int32)
    turns = bins[None, :] * (lags[:, None] + WIN) % WIN
    angles = turn_full / WIN * turns.astype(jnp.float32)
    weight = jnp.where(bins == 0, 1.0, 2.0).astype(jnp.float32) / (
        2.0 * math.sqrt(NBIN * windows_total)
    )
    return (jnp.cos(angles) * weight[None, :], jnp.sin(angles) * weight[None, :])


def whiten(frames, table, taper, band):
    values = frames.astype(jnp.float32)
    shaped = ((values - jnp.mean(values, axis=1, keepdims=True)) * taper[None, :]).astype(
        jnp.bfloat16
    )
    spec = jnp.dot(shaped, table, preferred_element_type=jnp.float32)
    real = spec[:, :NBIN]
    imag = spec[:, NBIN:]
    level = (
        jnp.dot(jnp.sqrt(real * real + imag * imag), band, precision=lax.Precision.HIGHEST) + 1e-05
    )
    return ((real / level).astype(jnp.bfloat16), (imag / level).astype(jnp.bfloat16))


def lag_factors(own_re, own_im, cos_w, sin_w):
    ar = own_re.astype(jnp.float32)[:, None, :]
    ai = own_im.astype(jnp.float32)[:, None, :]
    first = (ar * cos_w[None] - ai * sin_w[None]).astype(jnp.bfloat16)
    second = (ar * sin_w[None] + ai * cos_w[None]).astype(jnp.bfloat16)
    return first, second


def lag_terms(first, second, partner):
    return jnp.einsum(
        "ctf,kjf->tkcj", first, partner[:, 0], preferred_element_type=jnp.float32
    ) + jnp.einsum("ctf,kjf->tkcj", second, partner[:, 1], preferred_element_type=jnp.float32)


def split_for_win(corr):
    groups = lax.axis_size("win")
    return corr.reshape(groups, -1, *corr.shape[1:]).astype(jnp.bfloat16)


def pass_over_win(sent):
    return lax.all_to_all(sent, "win", split_axis=0, concat_axis=0, tiled=True)


def sum_over_win(arrived):
    return jnp.sum(arrived.astype(jnp.float32), axis=0)


def in_blocks(array, dim, size):
    before, after = (array.shape[:dim], array.shape[dim + 1 :])
    return jnp.moveaxis(array.reshape(*before, size, -1, *after), dim, 0)


def on_device(records, offsets, starts):
    n_chan = lax.axis_size("chan")
    groups = lax.axis_size("win")
    me = lax.axis_index("chan")
    frames = lax.dynamic_slice_in_dim(records, starts[0], WIN, 1)
    own_re, own_im = whiten(frames, dft_table(), taper_weights(), band_matrix())
    spectra = jnp.stack((own_re, own_im), axis=0)

    def shifted(by):
        pairs = [(i + by, i) for i in range(n_chan - by)]
        return lambda x: lax.ppermute(x, "chan", pairs)

    far = OFFCAP - 1
    farthest = shifted(far)(spectra)
    moves = [shifted(by) for by in range(1, far)]
    cos_w, sin_w = phase_tables(groups)
    first, second = lag_factors(own_re, own_im, cos_w, sin_w)
    hops = jnp.minimum(offsets, OFFCAP - offsets)
    key = jnp.where(offsets == far, -1, hops * OFFCAP + offsets)
    order = jnp.sort(key)[1:] % OFFCAP
    rank = jnp.sum(key[None, :] < key[:, None], axis=1)
    nearer = [lax.switch(order[k] - 1, moves, spectra) for k in range(K - 2)]
    early = jnp.stack([farthest] + nearer, axis=0)
    early_sent = lax.optimization_barrier(split_for_win(lag_terms(first, second, early)))

    def with_early(move):
        return lambda x, sent: (move(x), pass_over_win(sent))

    last, early_arrived = lax.switch(
        order[K - 2] - 1, [with_early(move) for move in moves], spectra, early_sent
    )
    last_sent = split_for_win(lag_terms(first, second, last[None]))
    early_sum = sum_over_win(early_arrived)
    last_sum = sum_over_win(pass_over_win(last_sent))
    by_rank = jnp.concatenate([early_sum, last_sum], axis=1)
    return jnp.take(by_rank, rank, axis=1)


def solution(mesh):
    in_specs = (P("chan", "win"), P(), P("win"))
    out_specs = P("win", None, "chan", None)
    return jax.shard_map(
        on_device, mesh=mesh, in_specs=in_specs, out_specs=out_specs, check_vma=False
    )
```

```python
import math

import jax
import jax.numpy as jnp
import ml_dtypes
import numpy as np
from jax import lax
from jax.sharding import PartitionSpec as P

WIN = 2048
NBIN = 1024
BAND = 64
L = 16
K = 4
OFFCAP = 16


turn_full = 2.0 * math.pi


def dft_table():
    samples = np.arange(WIN, dtype=np.int64)
    bins = np.arange(NBIN, dtype=np.int64)
    turns = samples[:, None] * bins[None, :] % WIN
    angles = np.float32(turn_full / WIN) * turns.astype(np.float32)
    table = np.concatenate([np.cos(angles), -np.sin(angles)], axis=1)
    return jnp.asarray(table.astype(ml_dtypes.bfloat16))


def taper_weights():
    samples = jnp.arange(WIN, dtype=jnp.float32)
    return 0.5 - 0.5 * jnp.cos(turn_full / WIN * (samples + 0.5))


def band_matrix():
    bins = jnp.arange(NBIN, dtype=jnp.int32)
    near = (jnp.abs(bins[:, None] - bins[None, :]) <= BAND).astype(jnp.float32)
    return near / jnp.sum(near, axis=0, keepdims=True)


def phase_tables(windows_total):
    lags = jnp.arange(L, dtype=jnp.int32) - L // 2
    bins = jnp.arange(NBIN, dtype=jnp.int32)
    turns = bins[None, :] * (lags[:, None] + WIN) % WIN
    angles = turn_full / WIN * turns.astype(jnp.float32)
    weight = jnp.where(bins == 0, 1.0, 2.0).astype(jnp.float32) / (
        2.0 * math.sqrt(NBIN * windows_total)
    )
    return (jnp.cos(angles) * weight[None, :], jnp.sin(angles) * weight[None, :])


def whiten(frames, table, taper, band):
    values = frames.astype(jnp.float32)
    shaped = ((values - jnp.mean(values, axis=1, keepdims=True)) * taper[None, :]).astype(
        jnp.bfloat16
    )
    spec = jnp.dot(shaped, table, preferred_element_type=jnp.float32)
    real = spec[:, :NBIN]
    imag = spec[:, NBIN:]
    level = (
        jnp.dot(jnp.sqrt(real * real + imag * imag), band, precision=lax.Precision.HIGH) + 1e-05
    )
    return ((real / level).astype(jnp.bfloat16), (imag / level).astype(jnp.bfloat16))


def lag_factors(own_re, own_im, cos_w, sin_w):
    ar = own_re.astype(jnp.float32)[:, None, :]
    ai = own_im.astype(jnp.float32)[:, None, :]
    first = (ar * cos_w[None] - ai * sin_w[None]).astype(jnp.bfloat16)
    second = (ar * sin_w[None] + ai * cos_w[None]).astype(jnp.bfloat16)
    return first, second


def lag_terms(first, second, partner):
    return jnp.einsum(
        "ctf,kjf->tkcj", first, partner[:, 0], preferred_element_type=jnp.float32
    ) + jnp.einsum("ctf,kjf->tkcj", second, partner[:, 1], preferred_element_type=jnp.float32)


def split_for_win(corr):
    groups = lax.axis_size("win")
    return corr.reshape(groups, -1, *corr.shape[1:]).astype(jnp.bfloat16)


def pass_over_win(sent):
    return lax.all_to_all(sent, "win", split_axis=0, concat_axis=0, tiled=True)


def sum_over_win(arrived):
    return jnp.sum(arrived.astype(jnp.float32), axis=0)


def in_blocks(array, dim, size):
    before, after = (array.shape[:dim], array.shape[dim + 1 :])
    return jnp.moveaxis(array.reshape(*before, size, -1, *after), dim, 0)


def on_device(records, offsets, starts):
    n_chan = lax.axis_size("chan")
    groups = lax.axis_size("win")
    me = lax.axis_index("chan")
    frames = lax.dynamic_slice_in_dim(records, starts[0], WIN, 1)
    hops = jnp.minimum(offsets, OFFCAP - offsets)
    key = jnp.where(offsets == OFFCAP - 1, -1, hops * OFFCAP + offsets)
    order = jnp.sort(key)[1:] % OFFCAP
    rank = jnp.sum(key[None, :] < key[:, None], axis=1)
    frames, order, rank = lax.optimization_barrier((frames, order, rank))
    own_re, own_im = whiten(frames, dft_table(), taper_weights(), band_matrix())
    spectra = jnp.stack((own_re, own_im), axis=0)

    def shifted(by):
        pairs = [(i + by, i) for i in range(n_chan - by)]
        return lambda x: lax.ppermute(x, "chan", pairs)

    far = OFFCAP - 1
    farthest = shifted(far)(spectra)
    moves = [shifted(by) for by in range(1, far)]
    cos_w, sin_w = phase_tables(groups)
    first, second = lag_factors(own_re, own_im, cos_w, sin_w)
    nearer = [lax.switch(order[k] - 1, moves, spectra) for k in range(K - 2)]
    early = jnp.stack([farthest] + nearer, axis=0)
    early_sent = lax.optimization_barrier(split_for_win(lag_terms(first, second, early)))

    def with_early(move):
        return lambda x, sent: (move(x), pass_over_win(sent))

    last, early_arrived = lax.switch(
        order[K - 2] - 1, [with_early(move) for move in moves], spectra, early_sent
    )
    last_sent = split_for_win(lag_terms(first, second, last[None]))
    early_sum = sum_over_win(early_arrived)
    last_sum = sum_over_win(pass_over_win(last_sent))
    by_rank = jnp.concatenate([early_sum, last_sum], axis=1)
    return jnp.take(by_rank, rank, axis=1)


def solution(mesh):
    in_specs = (P("chan", "win"), P(), P("win"))
    out_specs = P("win", None, "chan", None)
    return jax.shard_map(
        on_device, mesh=mesh, in_specs=in_specs, out_specs=out_specs, check_vma=False
    )
```

```python
import math

import jax
import jax.numpy as jnp
import ml_dtypes
import numpy as np
from jax import lax
from jax.sharding import PartitionSpec as P

WIN = 2048
NBIN = 1024
BAND = 64
L = 16
K = 4
OFFCAP = 16


turn_full = 2.0 * math.pi


def dft_table():
    samples = np.arange(WIN, dtype=np.int64)
    bins = np.arange(NBIN, dtype=np.int64)
    turns = samples[:, None] * bins[None, :] % WIN
    angles = np.float32(turn_full / WIN) * turns.astype(np.float32)
    table = np.concatenate([np.cos(angles), -np.sin(angles)], axis=1)
    return jnp.asarray(table.astype(ml_dtypes.bfloat16))


def taper_weights():
    samples = jnp.arange(WIN, dtype=jnp.float32)
    return 0.5 - 0.5 * jnp.cos(turn_full / WIN * (samples + 0.5))


def band_matrix():
    bins = jnp.arange(NBIN, dtype=jnp.int32)
    near = (jnp.abs(bins[:, None] - bins[None, :]) <= BAND).astype(jnp.float32)
    return near / jnp.sum(near, axis=0, keepdims=True)


def phase_tables(windows_total):
    lags = jnp.arange(L, dtype=jnp.int32) - L // 2
    bins = jnp.arange(NBIN, dtype=jnp.int32)
    turns = bins[None, :] * (lags[:, None] + WIN) % WIN
    angles = turn_full / WIN * turns.astype(jnp.float32)
    weight = jnp.where(bins == 0, 1.0, 2.0).astype(jnp.float32) / (
        2.0 * math.sqrt(NBIN * windows_total)
    )
    return (jnp.cos(angles) * weight[None, :], jnp.sin(angles) * weight[None, :])


def whiten(frames, table, taper, band):
    values = frames.astype(jnp.float32)
    shaped = ((values - jnp.mean(values, axis=1, keepdims=True)) * taper[None, :]).astype(
        jnp.bfloat16
    )
    spec = jnp.dot(shaped, table, preferred_element_type=jnp.float32)
    real = spec[:, :NBIN]
    imag = spec[:, NBIN:]
    level = (
        jnp.dot(jnp.sqrt(real * real + imag * imag), band, precision=lax.Precision.HIGH) + 1e-05
    )
    return ((real / level).astype(jnp.bfloat16), (imag / level).astype(jnp.bfloat16))


def lag_factors(own_re, own_im, cos_w, sin_w):
    ar = own_re.astype(jnp.float32)[:, None, :]
    ai = own_im.astype(jnp.float32)[:, None, :]
    first = (ar * cos_w[None] - ai * sin_w[None]).astype(jnp.bfloat16)
    second = (ar * sin_w[None] + ai * cos_w[None]).astype(jnp.bfloat16)
    return first, second


def lag_terms(first, second, partner):
    return jnp.einsum(
        "ctf,kjf->tkcj", first, partner[:, 0], preferred_element_type=jnp.float32
    ) + jnp.einsum("ctf,kjf->tkcj", second, partner[:, 1], preferred_element_type=jnp.float32)


def split_for_win(corr):
    groups = lax.axis_size("win")
    return corr.reshape(groups, -1, *corr.shape[1:]).astype(jnp.bfloat16)


def pass_over_win(sent):
    return lax.all_to_all(sent, "win", split_axis=0, concat_axis=0, tiled=True)


def sum_over_win(arrived):
    return jnp.sum(arrived.astype(jnp.float32), axis=0)


def in_blocks(array, dim, size):
    before, after = (array.shape[:dim], array.shape[dim + 1 :])
    return jnp.moveaxis(array.reshape(*before, size, -1, *after), dim, 0)


def on_device(records, offsets, starts):
    n_chan = lax.axis_size("chan")
    groups = lax.axis_size("win")
    me = lax.axis_index("chan")
    frames = lax.dynamic_slice_in_dim(records, starts[0], WIN, 1)
    hops = jnp.minimum(offsets, OFFCAP - offsets)
    key = jnp.where(offsets == OFFCAP - 1, -1, hops * OFFCAP + offsets)
    order = jnp.sort(key)[1:] % OFFCAP
    rank = jnp.sum(key[None, :] < key[:, None], axis=1)
    frames, order, rank = lax.optimization_barrier((frames, order, rank))
    own_re, own_im = whiten(frames, dft_table(), taper_weights(), band_matrix())
    spectra = jnp.stack((own_re, own_im), axis=0)

    def shifted(by):
        pairs = [(i + by, i) for i in range(n_chan - by)]
        return lambda x: lax.ppermute(x, "chan", pairs)

    far = OFFCAP - 1
    farthest = shifted(far)(spectra)
    moves = [shifted(by) for by in range(1, far)]
    cos_w, sin_w = phase_tables(groups)
    first, second = lag_factors(own_re, own_im, cos_w, sin_w)
    nearer = [lax.switch(order[k] - 1, moves, spectra) for k in range(K - 2)]
    early = jnp.stack(nearer, axis=0)
    early_sent = lax.optimization_barrier(split_for_win(lag_terms(first, second, early)))

    def with_early(move):
        return lambda x, sent: (move(x), pass_over_win(sent))

    last, early_arrived = lax.switch(
        order[K - 2] - 1, [with_early(move) for move in moves], spectra, early_sent
    )
    last_sent = split_for_win(lag_terms(first, second, jnp.stack([last, farthest], axis=0)))
    early_sum = sum_over_win(early_arrived)
    last_sum = sum_over_win(pass_over_win(last_sent))
    by_rank = jnp.concatenate([last_sum[:, 1:], early_sum, last_sum[:, :1]], axis=1)
    return jnp.take(by_rank, rank, axis=1)


def solution(mesh):
    in_specs = (P("chan", "win"), P(), P("win"))
    out_specs = P("win", None, "chan", None)
    return jax.shard_map(
        on_device, mesh=mesh, in_specs=in_specs, out_specs=out_specs, check_vma=False
    )
```

```python
import math

import jax
import jax.numpy as jnp
import ml_dtypes
import numpy as np
from jax import lax
from jax.sharding import PartitionSpec as P

WIN = 2048
NBIN = 1024
BAND = 64
L = 16
K = 4
OFFCAP = 16


turn_full = 2.0 * math.pi


def dft_table():
    samples = np.arange(WIN, dtype=np.int64)
    bins = np.arange(NBIN, dtype=np.int64)
    turns = samples[:, None] * bins[None, :] % WIN
    angles = np.float32(turn_full / WIN) * turns.astype(np.float32)
    table = np.concatenate([np.cos(angles), -np.sin(angles)], axis=1)
    return jnp.asarray(table.astype(ml_dtypes.bfloat16))


def taper_weights():
    samples = jnp.arange(WIN, dtype=jnp.float32)
    return 0.5 - 0.5 * jnp.cos(turn_full / WIN * (samples + 0.5))


def band_matrix():
    bins = jnp.arange(NBIN, dtype=jnp.int32)
    near = (jnp.abs(bins[:, None] - bins[None, :]) <= BAND).astype(jnp.float32)
    return near / jnp.sum(near, axis=0, keepdims=True)


def phase_tables(windows_total):
    lags = jnp.arange(L, dtype=jnp.int32) - L // 2
    bins = jnp.arange(NBIN, dtype=jnp.int32)
    turns = bins[None, :] * (lags[:, None] + WIN) % WIN
    angles = turn_full / WIN * turns.astype(jnp.float32)
    weight = jnp.where(bins == 0, 1.0, 2.0).astype(jnp.float32) / (
        2.0 * math.sqrt(NBIN * windows_total)
    )
    return (jnp.cos(angles) * weight[None, :], jnp.sin(angles) * weight[None, :])


def whiten(frames, table, taper, band):
    values = frames.astype(jnp.float32)
    shaped = ((values - jnp.mean(values, axis=1, keepdims=True)) * taper[None, :]).astype(
        jnp.bfloat16
    )
    spec = jnp.dot(shaped, table, preferred_element_type=jnp.float32)
    real = spec[:, :NBIN]
    imag = spec[:, NBIN:]
    level = (
        jnp.dot(jnp.sqrt(real * real + imag * imag), band, precision=lax.Precision.HIGH) + 1e-05
    )
    return ((real / level).astype(jnp.bfloat16), (imag / level).astype(jnp.bfloat16))


def lag_factors(own_re, own_im, cos_w, sin_w):
    ar = own_re.astype(jnp.float32)[:, None, :]
    ai = own_im.astype(jnp.float32)[:, None, :]
    first = (ar * cos_w[None] - ai * sin_w[None]).astype(jnp.bfloat16)
    second = (ar * sin_w[None] + ai * cos_w[None]).astype(jnp.bfloat16)
    return first, second


def lag_terms(first, second, partner):
    return jnp.einsum(
        "ctf,kjf->tkcj", first, partner[:, 0], preferred_element_type=jnp.float32
    ) + jnp.einsum("ctf,kjf->tkcj", second, partner[:, 1], preferred_element_type=jnp.float32)


def split_for_win(corr):
    groups = lax.axis_size("win")
    return corr.reshape(groups, -1, *corr.shape[1:]).astype(jnp.bfloat16)


def pass_over_win(sent):
    return lax.all_to_all(sent, "win", split_axis=0, concat_axis=0, tiled=True)


def sum_over_win(arrived):
    return jnp.sum(arrived.astype(jnp.float32), axis=0)


def in_blocks(array, dim, size):
    before, after = (array.shape[:dim], array.shape[dim + 1 :])
    return jnp.moveaxis(array.reshape(*before, size, -1, *after), dim, 0)


def on_device(records, offsets, starts):
    n_chan = lax.axis_size("chan")
    groups = lax.axis_size("win")
    me = lax.axis_index("chan")
    frames = lax.dynamic_slice_in_dim(records, starts[0], WIN, 1)
    hops = jnp.minimum(offsets, OFFCAP - offsets)
    key = jnp.where(offsets == OFFCAP - 1, -1, hops * OFFCAP + offsets)
    order = jnp.sort(key)[1:] % OFFCAP
    rank = jnp.sum(key[None, :] < key[:, None], axis=1)
    frames, order, rank = lax.optimization_barrier((frames, order, rank))
    own_re, own_im = whiten(frames, dft_table(), taper_weights(), band_matrix())
    spectra = jnp.stack((own_re, own_im), axis=0)

    def shifted(by):
        pairs = [(i + by, i) for i in range(n_chan - by)]
        return lambda x: lax.ppermute(x, "chan", pairs)

    far = OFFCAP - 1
    farthest = shifted(far)(spectra)
    moves = [shifted(by) for by in range(1, far)]
    cos_w, sin_w = phase_tables(groups)
    first, second = lag_factors(own_re, own_im, cos_w, sin_w)
    nearer = [lax.switch(order[k] - 1, moves, spectra) for k in range(K - 2)]
    early = jnp.stack([farthest] + nearer, axis=0)
    early_sent = lax.optimization_barrier(split_for_win(lag_terms(first, second, early)))

    def with_early(move):
        return lambda x, sent: (move(x), pass_over_win(sent))

    last, early_arrived = lax.switch(
        order[K - 2] - 1, [with_early(move) for move in moves], spectra, early_sent
    )
    last_sent = split_for_win(lag_terms(first, second, last[None]))
    early_sum = sum_over_win(early_arrived)
    last_sum = sum_over_win(pass_over_win(last_sent))
    slots = [
        jnp.where(
            rank[k] == K - 1,
            last_sum[:, 0],
            lax.dynamic_index_in_dim(early_sum, jnp.minimum(rank[k], K - 2), 1, keepdims=False),
        )
        for k in range(K)
    ]
    return jnp.stack(slots, axis=1)


def solution(mesh):
    in_specs = (P("chan", "win"), P(), P("win"))
    out_specs = P("win", None, "chan", None)
    return jax.shard_map(
        on_device, mesh=mesh, in_specs=in_specs, out_specs=out_specs, check_vma=False
    )
```

```python
import math

import jax
import jax.numpy as jnp
import ml_dtypes
import numpy as np
from jax import lax
from jax.sharding import PartitionSpec as P

WIN = 2048
NBIN = 1024
BAND = 64
L = 16
K = 4
OFFCAP = 16


turn_full = 2.0 * math.pi


def dft_table():
    samples = np.arange(WIN, dtype=np.int64)
    bins = np.arange(NBIN, dtype=np.int64)
    turns = samples[:, None] * bins[None, :] % WIN
    angles = np.float32(turn_full / WIN) * turns.astype(np.float32)
    table = np.concatenate([np.cos(angles), -np.sin(angles)], axis=1)
    return jnp.asarray(table.astype(ml_dtypes.bfloat16))


def taper_weights():
    samples = jnp.arange(WIN, dtype=jnp.float32)
    return 0.5 - 0.5 * jnp.cos(turn_full / WIN * (samples + 0.5))


def band_matrix():
    bins = jnp.arange(NBIN, dtype=jnp.int32)
    near = (jnp.abs(bins[:, None] - bins[None, :]) <= BAND).astype(jnp.float32)
    return near / jnp.sum(near, axis=0, keepdims=True)


def phase_tables(windows_total):
    lags = jnp.arange(L, dtype=jnp.int32) - L // 2
    bins = jnp.arange(NBIN, dtype=jnp.int32)
    turns = bins[None, :] * (lags[:, None] + WIN) % WIN
    angles = turn_full / WIN * turns.astype(jnp.float32)
    weight = jnp.where(bins == 0, 1.0, 2.0).astype(jnp.float32) / (
        2.0 * math.sqrt(NBIN * windows_total)
    )
    return (jnp.cos(angles) * weight[None, :], jnp.sin(angles) * weight[None, :])


def whiten(frames, table, taper, band):
    values = frames.astype(jnp.float32)
    shaped = ((values - jnp.mean(values, axis=1, keepdims=True)) * taper[None, :]).astype(
        jnp.bfloat16
    )
    spec = jnp.dot(shaped, table, preferred_element_type=jnp.float32)
    real = spec[:, :NBIN]
    imag = spec[:, NBIN:]
    level = (
        jnp.dot(jnp.sqrt(real * real + imag * imag), band, precision=lax.Precision.HIGH) + 1e-05
    )
    return ((real / level).astype(jnp.bfloat16), (imag / level).astype(jnp.bfloat16))


def lag_factors(own_re, own_im, cos_w, sin_w):
    ar = own_re.astype(jnp.float32)[:, None, :]
    ai = own_im.astype(jnp.float32)[:, None, :]
    first = (ar * cos_w[None] - ai * sin_w[None]).astype(jnp.bfloat16)
    second = (ar * sin_w[None] + ai * cos_w[None]).astype(jnp.bfloat16)
    return first, second


def lag_terms(first, second, partner):
    return jnp.einsum(
        "ctf,kjf->tkcj", first, partner[:, 0], preferred_element_type=jnp.float32
    ) + jnp.einsum("ctf,kjf->tkcj", second, partner[:, 1], preferred_element_type=jnp.float32)


def split_for_win(corr):
    groups = lax.axis_size("win")
    return corr.reshape(groups, -1, *corr.shape[1:]).astype(jnp.bfloat16)


def pass_over_win(sent):
    return lax.all_to_all(sent, "win", split_axis=0, concat_axis=0, tiled=True)


def sum_over_win(arrived):
    return jnp.sum(arrived.astype(jnp.float32), axis=0)


def in_blocks(array, dim, size):
    before, after = (array.shape[:dim], array.shape[dim + 1 :])
    return jnp.moveaxis(array.reshape(*before, size, -1, *after), dim, 0)


def on_device(records, offsets, starts):
    n_chan = lax.axis_size("chan")
    groups = lax.axis_size("win")
    me = lax.axis_index("chan")
    frames = lax.dynamic_slice_in_dim(records, starts[0], WIN, 1)
    hops = jnp.minimum(offsets, OFFCAP - offsets)
    key = jnp.where(offsets == OFFCAP - 1, -1, hops * OFFCAP + offsets)
    order = jnp.sort(key)[1:] % OFFCAP
    rank = jnp.sum(key[None, :] < key[:, None], axis=1)
    frames, order, rank = lax.optimization_barrier((frames, order, rank))
    own_re, own_im = whiten(frames, dft_table(), taper_weights(), band_matrix())
    spectra = jnp.stack((own_re, own_im), axis=0)

    def shifted(by):
        pairs = [(i + by, i) for i in range(n_chan - by)]
        return lambda x: lax.ppermute(x, "chan", pairs)

    far = OFFCAP - 1
    farthest = shifted(far)(spectra)
    moves = [shifted(by) for by in range(1, far)]
    cos_w, sin_w = phase_tables(groups)
    first, second = lag_factors(own_re, own_im, cos_w, sin_w)
    nearer = [lax.switch(order[k] - 1, moves, spectra) for k in (0, K - 2)]
    early = jnp.stack([farthest] + nearer, axis=0)
    early_sent = lax.optimization_barrier(split_for_win(lag_terms(first, second, early)))

    def with_early(move):
        return lambda x, sent: (move(x), pass_over_win(sent))

    last, early_arrived = lax.switch(
        order[1] - 1, [with_early(move) for move in moves], spectra, early_sent
    )
    last_sent = split_for_win(lag_terms(first, second, last[None]))
    early_sum = sum_over_win(early_arrived)
    last_sum = sum_over_win(pass_over_win(last_sent))
    place = jnp.array([0, 1, 3, 2], jnp.int32)[rank]
    slots = [
        jnp.where(
            place[k] == K - 1,
            last_sum[:, 0],
            lax.dynamic_index_in_dim(early_sum, jnp.minimum(place[k], K - 2), 1, keepdims=False),
        )
        for k in range(K)
    ]
    return jnp.stack(slots, axis=1)


def solution(mesh):
    in_specs = (P("chan", "win"), P(), P("win"))
    out_specs = P("win", None, "chan", None)
    return jax.shard_map(
        on_device, mesh=mesh, in_specs=in_specs, out_specs=out_specs, check_vma=False
    )
```

```python
import math

import jax
import jax.numpy as jnp
import ml_dtypes
import numpy as np
from jax import lax
from jax.sharding import PartitionSpec as P

WIN = 2048
NBIN = 1024
BAND = 64
L = 16
K = 4
OFFCAP = 16


turn_full = 2.0 * math.pi


def dft_table():
    samples = np.arange(WIN, dtype=np.int64)
    bins = np.arange(NBIN, dtype=np.int64)
    turns = samples[:, None] * bins[None, :] % WIN
    angles = np.float32(turn_full / WIN) * turns.astype(np.float32)
    table = np.concatenate([np.cos(angles), -np.sin(angles)], axis=1)
    return jnp.asarray(table.astype(ml_dtypes.bfloat16))


def taper_weights():
    samples = jnp.arange(WIN, dtype=jnp.float32)
    return 0.5 - 0.5 * jnp.cos(turn_full / WIN * (samples + 0.5))


def band_matrix():
    bins = jnp.arange(NBIN, dtype=jnp.int32)
    near = (jnp.abs(bins[:, None] - bins[None, :]) <= BAND).astype(jnp.float32)
    return near / jnp.sum(near, axis=0, keepdims=True)


def phase_tables(windows_total):
    lags = jnp.arange(L, dtype=jnp.int32) - L // 2
    bins = jnp.arange(NBIN, dtype=jnp.int32)
    turns = bins[None, :] * (lags[:, None] + WIN) % WIN
    angles = turn_full / WIN * turns.astype(jnp.float32)
    weight = jnp.where(bins == 0, 1.0, 2.0).astype(jnp.float32) / (
        2.0 * math.sqrt(NBIN * windows_total)
    )
    return (jnp.cos(angles) * weight[None, :], jnp.sin(angles) * weight[None, :])


def whiten(frames, table, taper, band):
    values = frames.astype(jnp.float32)
    shaped = ((values - jnp.mean(values, axis=1, keepdims=True)) * taper[None, :]).astype(
        jnp.bfloat16
    )
    spec = jnp.dot(shaped, table, preferred_element_type=jnp.float32)
    real = spec[:, :NBIN]
    imag = spec[:, NBIN:]
    level = (
        jnp.dot(jnp.sqrt(real * real + imag * imag), band, precision=lax.Precision.HIGH) + 1e-05
    )
    return ((real / level).astype(jnp.bfloat16), (imag / level).astype(jnp.bfloat16))


def lag_factors(own_re, own_im, cos_w, sin_w):
    ar = own_re.astype(jnp.float32)[:, None, :]
    ai = own_im.astype(jnp.float32)[:, None, :]
    first = (ar * cos_w[None] - ai * sin_w[None]).astype(jnp.bfloat16)
    second = (ar * sin_w[None] + ai * cos_w[None]).astype(jnp.bfloat16)
    return first, second


def lag_terms(first, second, partner):
    return jnp.einsum(
        "ctf,kjf->tkcj", first, partner[:, 0], preferred_element_type=jnp.float32
    ) + jnp.einsum("ctf,kjf->tkcj", second, partner[:, 1], preferred_element_type=jnp.float32)


def split_for_win(corr):
    groups = lax.axis_size("win")
    return corr.reshape(groups, -1, *corr.shape[1:]).astype(jnp.bfloat16)


def pass_over_win(sent):
    return lax.all_to_all(sent, "win", split_axis=0, concat_axis=0, tiled=True)


def sum_over_win(arrived):
    return jnp.sum(arrived.astype(jnp.float32), axis=0)


def in_blocks(array, dim, size):
    before, after = (array.shape[:dim], array.shape[dim + 1 :])
    return jnp.moveaxis(array.reshape(*before, size, -1, *after), dim, 0)


def on_device(records, offsets, starts):
    n_chan = lax.axis_size("chan")
    groups = lax.axis_size("win")
    me = lax.axis_index("chan")
    frames = lax.dynamic_slice_in_dim(records, starts[0], WIN, 1)
    own_re, own_im = whiten(frames, dft_table(), taper_weights(), band_matrix())
    spectra = jnp.stack((own_re, own_im), axis=0)

    def shifted(by):
        pairs = [(i + by, i) for i in range(n_chan - by)]
        return lambda x: lax.ppermute(x, "chan", pairs)

    far = OFFCAP - 1
    farthest = shifted(far)(spectra)
    moves = [shifted(by) for by in range(1, far)]
    cos_w, sin_w = phase_tables(groups)
    first, second = lag_factors(own_re, own_im, cos_w, sin_w)
    hops = jnp.minimum(offsets, OFFCAP - offsets)
    key = jnp.where(offsets == far, -1, hops * OFFCAP + offsets)
    order = jnp.sort(key)[1:] % OFFCAP
    rank = jnp.sum(key[None, :] < key[:, None], axis=1)
    nearer = [lax.switch(order[k] - 1, moves, spectra) for k in range(K - 2)]
    early = jnp.stack([farthest] + nearer, axis=0)
    early_sent = lax.optimization_barrier(split_for_win(lag_terms(first, second, early)))

    def with_early(move):
        return lambda x, sent: (move(x), pass_over_win(sent))

    last, early_arrived = lax.switch(
        order[K - 2] - 1, [with_early(move) for move in moves], spectra, early_sent
    )
    last_sent = split_for_win(lag_terms(first, second, last[None]))
    early_sum = sum_over_win(early_arrived)
    last_sum = sum_over_win(pass_over_win(last_sent))
    by_rank = jnp.concatenate([early_sum, last_sum], axis=1)
    return jnp.take(by_rank, rank, axis=1)


def solution(mesh):
    in_specs = (P("chan", "win"), P(), P("win"))
    out_specs = P("win", None, "chan", None)
    return jax.shard_map(
        on_device, mesh=mesh, in_specs=in_specs, out_specs=out_specs, check_vma=False
    )
```

```python
import math

import jax
import jax.numpy as jnp
import ml_dtypes
import numpy as np
from jax import lax
from jax.sharding import PartitionSpec as P

WIN = 2048
NBIN = 1024
BAND = 64
L = 16
K = 4
OFFCAP = 16


turn_full = 2.0 * math.pi


def dft_table():
    samples = np.arange(WIN, dtype=np.int64)
    bins = np.arange(NBIN, dtype=np.int64)
    turns = samples[:, None] * bins[None, :] % WIN
    angles = np.float32(turn_full / WIN) * turns.astype(np.float32)
    table = np.concatenate([np.cos(angles), -np.sin(angles)], axis=1)
    return jnp.asarray(table.astype(ml_dtypes.bfloat16))


def taper_weights():
    samples = jnp.arange(WIN, dtype=jnp.float32)
    return 0.5 - 0.5 * jnp.cos(turn_full / WIN * (samples + 0.5))


def band_matrix():
    bins = jnp.arange(NBIN, dtype=jnp.int32)
    near = (jnp.abs(bins[:, None] - bins[None, :]) <= BAND).astype(jnp.float32)
    return near / jnp.sum(near, axis=0, keepdims=True)


def phase_tables(windows_total):
    lags = jnp.arange(L, dtype=jnp.int32) - L // 2
    bins = jnp.arange(NBIN, dtype=jnp.int32)
    turns = bins[None, :] * (lags[:, None] + WIN) % WIN
    angles = turn_full / WIN * turns.astype(jnp.float32)
    weight = jnp.where(bins == 0, 1.0, 2.0).astype(jnp.float32) / (
        2.0 * math.sqrt(NBIN * windows_total)
    )
    return (jnp.cos(angles) * weight[None, :], jnp.sin(angles) * weight[None, :])


def whiten(frames, table, taper, band):
    values = frames.astype(jnp.float32)
    shaped = ((values - jnp.mean(values, axis=1, keepdims=True)) * taper[None, :]).astype(
        jnp.bfloat16
    )
    spec = jnp.dot(shaped, table, preferred_element_type=jnp.float32)
    real = spec[:, :NBIN]
    imag = spec[:, NBIN:]
    level = (
        jnp.dot(jnp.sqrt(real * real + imag * imag), band, precision=lax.Precision.HIGHEST) + 1e-05
    )
    return ((real / level).astype(jnp.bfloat16), (imag / level).astype(jnp.bfloat16))


def lag_factors(own_re, own_im, cos_w, sin_w):
    ar = own_re.astype(jnp.float32)[:, None, :]
    ai = own_im.astype(jnp.float32)[:, None, :]
    first = (ar * cos_w[None] - ai * sin_w[None]).astype(jnp.bfloat16)
    second = (ar * sin_w[None] + ai * cos_w[None]).astype(jnp.bfloat16)
    return first, second


def lag_terms(first, second, partner):
    return jnp.einsum(
        "ctf,kjf->tkcj", first, partner[:, 0], preferred_element_type=jnp.float32
    ) + jnp.einsum("ctf,kjf->tkcj", second, partner[:, 1], preferred_element_type=jnp.float32)


def split_for_win(corr):
    groups = lax.axis_size("win")
    return corr.reshape(groups, -1, *corr.shape[1:]).astype(jnp.bfloat16)


def pass_over_win(sent):
    return lax.all_to_all(sent, "win", split_axis=0, concat_axis=0, tiled=True)


def sum_over_win(arrived):
    return jnp.sum(arrived.astype(jnp.float32), axis=0)


def in_blocks(array, dim, size):
    before, after = (array.shape[:dim], array.shape[dim + 1 :])
    return jnp.moveaxis(array.reshape(*before, size, -1, *after), dim, 0)


def on_device(records, offsets, starts):
    n_chan = lax.axis_size("chan")
    groups = lax.axis_size("win")
    me = lax.axis_index("chan")
    frames = lax.dynamic_slice_in_dim(records, starts[0], WIN, 1)
    own_re, own_im = whiten(frames, dft_table(), taper_weights(), band_matrix())
    spectra = jnp.stack((own_re, own_im), axis=0)

    def shifted(by):
        pairs = [(i + by, i) for i in range(n_chan - by)]
        return lambda x: lax.ppermute(x, "chan", pairs)

    far = OFFCAP - 1
    farthest = shifted(far)(spectra)
    moves = [shifted(by) for by in range(1, far)]
    cos_w, sin_w = phase_tables(groups)
    first, second = lag_factors(own_re, own_im, cos_w, sin_w)
    hops = jnp.minimum(offsets, OFFCAP - offsets)
    key = jnp.where(offsets == far, -1, hops * OFFCAP + offsets)
    order = jnp.sort(key)[1:] % OFFCAP
    rank = jnp.sum(key[None, :] < key[:, None], axis=1)
    nearer = [lax.switch(order[k] - 1, moves, spectra) for k in range(K - 2)]
    early = jnp.stack([farthest] + nearer, axis=0)
    early_sent = lax.optimization_barrier(split_for_win(lag_terms(first, second, early)))

    def with_early(move):
        return lambda x, sent: (move(x), pass_over_win(sent))

    last, early_arrived = lax.switch(
        order[K - 2] - 1, [with_early(move) for move in moves], spectra, early_sent
    )
    last_sent = split_for_win(lag_terms(first, second, last[None]))
    early_sum = sum_over_win(early_arrived)
    last_sum = sum_over_win(pass_over_win(last_sent))
    slots = [
        jnp.where(
            rank[k] == K - 1,
            last_sum[:, 0],
            lax.dynamic_index_in_dim(early_sum, jnp.minimum(rank[k], K - 2), 1, keepdims=False),
        )
        for k in range(K)
    ]
    return jnp.stack(slots, axis=1)


def solution(mesh):
    in_specs = (P("chan", "win"), P(), P("win"))
    out_specs = P("win", None, "chan", None)
    return jax.shard_map(
        on_device, mesh=mesh, in_specs=in_specs, out_specs=out_specs, check_vma=False
    )
```
